128 devices in a mesh: kv: 16 (over y, x), seq: 8 (over z, core).
Axes of the slice: x: 4, y: 4, z: 4, core: 2. Of those that a mesh axis runs over, the one named last changes fastest.
Arguments:
- prefill_keys: bfloat16 [262144, 1024], P(('kv', 'seq')), may hold values from -50 to 50
- queries: bfloat16 [1024, 8192], P('seq'), may hold values from -6 to 6
- outlier_spans: int32 [512], P(('kv', 'seq')), may hold values from 0 to 255
- start_basis: float32 [160, 1024], replicated, may hold values from -6 to 6
Outputs:
- basis: float32 [160, 1024], replicated
- coefficients: bfloat16 [160, 262144], P(None, ('kv', 'seq'))
- landmark_scores: bfloat16 [8, 1024, 32768], P(None, 'seq', 'kv')
- outlier_scores: bfloat16 [8, 1024, 4096], P(None, 'seq', 'kv')
The draws below stay inside these ranges and needn't reach their ends.
Inputs may be any that keep to these rules, and one draw needn't show every extreme that they name: `outlier_spans`: entries index spans of 8 rows among the rows held by the same device.
All inputs are finite; a program needn't handle non-finite values.
Results may differ from the reference program's by a relative error of at most 0.0037.
Values may be sent and summed in bfloat16 or wider, within the bound.
No kernel may reach another device: no remote copies, remote signals or barrier semaphores. Data moves between devices by JAX's collectives and lax.ppermute only.
A program may use at most 128 MiB of HBM per device.

```python
import math
import jax
import jax.numpy as jnp
from jax import lax

KVH = 8
HEAD = 128
GROUP = 8
D = 1024
RANK = 160
ITERS = 8
SPAN = 8
OUT_DEV = 4
QROWS = 128
ROWS_DEV = 2048
TOKENS = 262144
NCHUNK = 32768
NOUT = 512
NQ = 1024


def draw_prefill_keys(key, part):
    key_latent, key_mixing, key_noise, key_column, key_row = jax.random.split(jax.random.fold_in(key, 17), 5)
    latent_width = RANK * 6 // 5
    position = jnp.arange(latent_width).astype(jnp.float32)
    strength = 3.0 / (1.0 + position * 8.0 / RANK)
    mixing = jax.random.normal(key_mixing, (latent_width, D), jnp.float32) / jnp.sqrt(jnp.float32(latent_width))
    column_scale = jnp.exp(jax.random.uniform(key_column, (D,), jnp.float32, -0.7, 0.7))
    latent = jnp.clip(jax.random.normal(key_latent, (TOKENS, latent_width), jnp.float32), -5.0, 5.0)
    noise = 0.15 * jnp.clip(jax.random.normal(key_noise, (TOKENS, D), jnp.float32), -5.0, 5.0)
    row_scale = jnp.exp(jax.random.uniform(key_row, (TOKENS, 1), jnp.float32, -1.15, 1.15))
    shaped = jnp.dot(latent * strength, mixing, precision=lax.Precision.HIGHEST, preferred_element_type=jnp.float32)
    keys = (shaped + noise) * column_scale * row_scale
    return jnp.clip(keys, -48.0, 48.0).astype(jnp.bfloat16)


def touch_ends(result, own_key, least, largest):
    spot = [jax.random.randint(jax.random.fold_in(own_key, axis), (), 0, length) for axis, length in enumerate(result.shape)]
    main_axis = result.shape.index(max(result.shape))
    beside = spot[:main_axis] + [(spot[main_axis] + 1) % result.shape[main_axis]] + spot[main_axis + 1:]
    return result.at[tuple(spot)].set(least).at[tuple(beside)].set(largest)


def levels(rng, shape, cuts, least, top_value):
    loudness = 1.0
    for axis_at, shards_of in cuts:
        steps = jax.random.uniform(jax.random.fold_in(jax.random.fold_in(rng, 6), axis_at), (shards_of,), jnp.float32, least / len(cuts), top_value / len(cuts))
        loudness = loudness * jnp.repeat(jnp.exp(steps), shape[axis_at] // shards_of).reshape((-1,) + (1,) * (len(shape) - 1 - axis_at))
    return loudness


def gaussian(own_key, extent, deviation, bound, cuts=(), held_as=jnp.bfloat16):
    loudness = levels(own_key, extent, cuts, -0.22, 0.18) if cuts else 1.0
    drawn = jax.random.normal(own_key, extent, jnp.float32) * deviation * loudness
    return jnp.minimum(jnp.maximum(drawn, -bound), bound).astype(held_as)


def setup_inputs(seed: int = 0) -> dict:
    key_list = jax.random.split(jax.random.key(seed), 5)
    return {
        "prefill_keys": draw_prefill_keys(jax.random.fold_in(key_list[4], 71), 0),
        "queries": gaussian(key_list[1], (NQ, KVH * GROUP * HEAD), 1.0, 6.0, ((0, 8),)),
        "outlier_spans": touch_ends(jax.random.randint(key_list[2], (NOUT,), 0, ROWS_DEV // SPAN), jax.random.fold_in(key_list[2], 1), 0, (ROWS_DEV // SPAN) - 1).astype(jnp.int32),
        "start_basis": gaussian(key_list[3], (RANK, D), 1.0, 6.0, (), jnp.float32),
    }


def cholesky_pass(product):
    highest = lax.Precision.HIGHEST
    moment = jnp.dot(product.astype(jnp.float32), product.T.astype(jnp.float32), precision=highest, preferred_element_type=jnp.float32)
    factor = jnp.linalg.cholesky(moment)
    return jax.scipy.linalg.solve_triangular(factor, product, lower=True)

def group_scores(queries, key_rows):
    count_rows = key_rows.shape[0]
    scale_factor = 1.0 / math.sqrt(HEAD)
    query_heads = jnp.transpose(queries.reshape(NQ // QROWS, QROWS, KVH, GROUP, HEAD), (2, 0, 1, 3, 4))
    key_heads = jnp.transpose(key_rows.reshape(count_rows, KVH, HEAD), (1, 0, 2))

    def one_head(pairing):
        query_group, key_group = pairing
        key_float = key_group.astype(jnp.float32)

        def one_block(query_block):
            scores = jnp.einsum('qgd,cd->qgc', query_block.astype(jnp.float32), key_float, precision=lax.Precision.HIGHEST)
            return (lax.optimization_barrier(jnp.max(scores, axis=1)) * scale_factor).astype(jnp.bfloat16)
        return lax.map(one_block, query_group).reshape(NQ, count_rows)
    return lax.map(one_head, (query_heads, key_heads))

def reference(prefill_keys, queries, outlier_spans, start_basis):
    highest = lax.Precision.HIGHEST
    block_rows = math.gcd(TOKENS, 8192)

    def add_block(running, rows_block):
        rows_float = rows_block.astype(jnp.float32)
        return (running + jnp.dot(rows_float.T.astype(jnp.float32), rows_float.astype(jnp.float32), precision=highest, preferred_element_type=jnp.float32), None)
    gram_sum, unused = lax.scan(add_block, jnp.zeros((D, D), jnp.float32), prefill_keys.reshape(TOKENS // block_rows, block_rows, D))
    gram = gram_sum / TOKENS
    subspace = start_basis
    for iteration in range(ITERS):
        product = jnp.dot(subspace.astype(jnp.float32), gram.astype(jnp.float32), precision=highest, preferred_element_type=jnp.float32)
        subspace = cholesky_pass(product)
    rounded = subspace.astype(jnp.bfloat16)
    coefficients = lax.dot_general(rounded.astype(jnp.float32), prefill_keys.astype(jnp.float32), (((1,), (1,)), ((), ())), preferred_element_type=jnp.float32).astype(jnp.bfloat16)
    spanned = prefill_keys.reshape(NCHUNK, SPAN, D)
    landmarks = lax.optimization_barrier(jnp.mean(spanned.astype(jnp.float32), axis=1)).astype(jnp.bfloat16)
    owners = jnp.arange(NOUT, dtype=jnp.int32) // OUT_DEV
    global_spans = (owners * (ROWS_DEV // SPAN) + outlier_spans).astype(jnp.int32)
    picked = jnp.take(spanned, global_spans, axis=0).reshape(NOUT * SPAN, D)
    landmark_scores = group_scores(queries, landmarks)
    outlier_scores = group_scores(queries, picked)
    return (subspace, coefficients, landmark_scores, outlier_scores)
```

```python
import math

import jax
import jax.numpy as jnp
from jax import lax
from jax.sharding import PartitionSpec as P

KVH = 8
HEAD = 128
GROUP = 8
ITERS = 8
SPAN = 8


def moment_of(product):
    return jnp.dot(
        product, product.T, precision=lax.Precision.HIGHEST, preferred_element_type=jnp.float32
    )


def solve_lower(moment, product):
    return jax.scipy.linalg.solve_triangular(jnp.linalg.cholesky(moment), product, lower=True)


def apply_gram(subspace, gram):
    return jnp.dot(
        subspace, gram, precision=lax.Precision.HIGHEST, preferred_element_type=jnp.float32
    )


def local(prefill_keys, queries, outlier_spans, start_basis):
    rows_dev = prefill_keys.shape[0]
    width = prefill_keys.shape[1]
    inverse_tokens = 1.0 / (rows_dev * lax.axis_size("kv") * lax.axis_size("seq"))
    scale_factor = 1.0 / math.sqrt(HEAD)
    spanned = prefill_keys.reshape(rows_dev // SPAN, SPAN, width)
    landmarks = jnp.mean(spanned, axis=1, dtype=jnp.float32).astype(jnp.bfloat16)
    picked = jnp.take(spanned, outlier_spans, axis=0).reshape(-1, width)
    query_count = queries.shape[0]
    query_heads = jnp.transpose(queries.reshape(query_count, KVH, GROUP, HEAD), (1, 0, 2, 3))

    def score_rows(shard_rows):
        count_rows = shard_rows.shape[0]
        key_heads = jnp.swapaxes(shard_rows.reshape(count_rows, KVH, HEAD), 0, 1)

        def one_head(pairing):
            query_group, key_group = pairing
            scores = jnp.einsum(
                "qgd,cd->qgc", query_group, key_group, preferred_element_type=jnp.float32
            )
            return jnp.max(scores, axis=1)

        return (lax.map(one_head, (query_heads, key_heads)) * scale_factor).astype(jnp.bfloat16)

    landmark_scores = score_rows(lax.all_gather(landmarks, "seq", axis=0, tiled=True))
    outlier_scores = score_rows(lax.all_gather(picked, "seq", axis=0, tiled=True))
    gram = lax.psum(
        lax.dot_general(
            prefill_keys, prefill_keys, (((0,), (0,)), ((), ())), preferred_element_type=jnp.float32
        ),
        ("kv", "seq"),
    ) * inverse_tokens
    subspace = start_basis
    for iteration in range(ITERS):
        product = apply_gram(subspace, gram)
        subspace = solve_lower(moment_of(product), product)
    rounded = subspace.astype(jnp.bfloat16)
    coefficients = lax.dot_general(
        rounded, prefill_keys, (((1,), (1,)), ((), ())), preferred_element_type=jnp.float32
    ).astype(jnp.bfloat16)
    return (subspace, coefficients, landmark_scores, outlier_scores)


def solution(mesh):
    placed = (P(("kv", "seq"), None), P("seq", None), P(("kv", "seq")), P())
    return jax.shard_map(
        local,
        mesh=mesh,
        in_specs=placed,
        out_specs=(P(), P(None, ("kv", "seq")), P(None, "seq", "kv"), P(None, "seq", "kv")),
        check_vma=False,
    )
```

```python
import math

import jax
import jax.numpy as jnp
from jax import lax
from jax.experimental import pallas as pl
from jax.sharding import PartitionSpec as P

HI = lax.Precision.HIGHEST

KVH = 8
HEAD = 128
GROUP = 8
ITERS = 8
SPAN = 8


def moment_of(product):
    return jnp.dot(
        product, product.T, precision=lax.Precision.HIGHEST, preferred_element_type=jnp.float32
    )


def _mm(a, b):
    return jnp.dot(a, b, precision=HI, preferred_element_type=jnp.float32)

def _mm_nt(a, b):
    return lax.dot_general(a, b, (((1,), (1,)), ((), ())), precision=HI,
                           preferred_element_type=jnp.float32)

def _eliminate(a):
    n = a.shape[0]
    rows = lax.broadcasted_iota(jnp.int32, (n, 1), 0)
    eye = lax.broadcasted_iota(jnp.int32, (n, n), 0) == lax.broadcasted_iota(jnp.int32, (n, n), 1)
    e = eye.astype(jnp.float32)
    for j in range(n):
        inv = 1.0 / a[j:j + 1, j:j + 1]
        f = jnp.where(rows > j, a[:, j:j + 1] * inv, 0.0)
        a = a - f * a[j:j + 1, :]
        e = e - f * e[j:j + 1, :]
    diag = jnp.where(eye, a, 0.0)
    return e, jnp.sum(diag, axis=1, keepdims=True), jnp.sum(diag, axis=0, keepdims=True)

def _cholqr_kernel(m_ref, p_ref, o_ref):
    h = 128
    e0, d0c, d0r = _eliminate(m_ref[0:h, 0:h])
    c = _mm_nt(m_ref[h:, 0:h], e0) / d0r
    s = m_ref[h:, h:] - _mm_nt(c * d0r, c)
    e1, d1c, _ = _eliminate(s)
    q0 = _mm(e0, p_ref[0:h, :])
    q1 = _mm(e1, p_ref[h:, :] - _mm(c, q0))
    o_ref[0:h, :] = q0 * lax.rsqrt(d0c)
    o_ref[h:, :] = q1 * lax.rsqrt(d1c)

def solve_lower(moment, product):
    return pl.pallas_call(
        _cholqr_kernel, out_shape=jax.ShapeDtypeStruct(product.shape, jnp.float32)
    )(moment, product)


def apply_gram(subspace, gram):
    return jnp.dot(
        subspace, gram, precision=lax.Precision.HIGHEST, preferred_element_type=jnp.float32
    )


def local(prefill_keys, queries, outlier_spans, start_basis):
    rows_dev = prefill_keys.shape[0]
    width = prefill_keys.shape[1]
    inverse_tokens = 1.0 / (rows_dev * lax.axis_size("kv") * lax.axis_size("seq"))
    scale_factor = 1.0 / math.sqrt(HEAD)
    spanned = prefill_keys.reshape(rows_dev // SPAN, SPAN, width)
    landmarks = jnp.mean(spanned, axis=1, dtype=jnp.float32).astype(jnp.bfloat16)
    picked = jnp.take(spanned, outlier_spans, axis=0).reshape(-1, width)
    query_count = queries.shape[0]
    query_heads = jnp.transpose(queries.reshape(query_count, KVH, GROUP, HEAD), (1, 0, 2, 3))

    def score_rows(shard_rows):
        count_rows = shard_rows.shape[0]
        key_heads = jnp.swapaxes(shard_rows.reshape(count_rows, KVH, HEAD), 0, 1)

        def one_head(pairing):
            query_group, key_group = pairing
            scores = jnp.einsum(
                "qgd,cd->qgc", query_group, key_group, preferred_element_type=jnp.float32
            )
            return jnp.max(scores, axis=1)

        return (lax.map(one_head, (query_heads, key_heads)) * scale_factor).astype(jnp.bfloat16)

    landmark_scores = score_rows(lax.all_gather(landmarks, "seq", axis=0, tiled=True))
    outlier_scores = score_rows(lax.all_gather(picked, "seq", axis=0, tiled=True))
    gram = lax.psum(
        lax.dot_general(
            prefill_keys, prefill_keys, (((0,), (0,)), ((), ())), preferred_element_type=jnp.float32
        ),
        ("kv", "seq"),
    ) * inverse_tokens
    subspace = start_basis
    for iteration in range(ITERS):
        product = apply_gram(subspace, gram)
        subspace = solve_lower(moment_of(product), product)
    rounded = subspace.astype(jnp.bfloat16)
    coefficients = lax.dot_general(
        rounded, prefill_keys, (((1,), (1,)), ((), ())), preferred_element_type=jnp.float32
    ).astype(jnp.bfloat16)
    return (subspace, coefficients, landmark_scores, outlier_scores)


def solution(mesh):
    placed = (P(("kv", "seq"), None), P("seq", None), P(("kv", "seq")), P())
    return jax.shard_map(
        local,
        mesh=mesh,
        in_specs=placed,
        out_specs=(P(), P(None, ("kv", "seq")), P(None, "seq", "kv"), P(None, "seq", "kv")),
        check_vma=False,
    )
```

```python
import math

import jax
import jax.numpy as jnp
from jax import lax
from jax.experimental import pallas as pl
from jax.experimental.pallas import tpu as pltpu
from jax.sharding import PartitionSpec as P

HI = lax.Precision.HIGHEST
HALF = 128

KVH = 8
HEAD = 128
GROUP = 8
ITERS = 8
SPAN = 8


def _mm(a, b):
    return jnp.dot(a, b, precision=HI, preferred_element_type=jnp.float32)


def _mm_nt(a, b):
    return lax.dot_general(
        a, b, (((1,), (1,)), ((), ())), precision=HI, preferred_element_type=jnp.float32
    )


def _eliminate(a_ref, e_ref):
    n = a_ref.shape[0]
    eye = lax.broadcasted_iota(jnp.int32, (n, n), 0) == lax.broadcasted_iota(jnp.int32, (n, n), 1)
    e_ref[...] = eye.astype(jnp.float32)
    for j in range(n):
        low = (j // 8) * 8
        row_a = a_ref[j:j + 1, :]
        inv = 1.0 / row_a[:, j:j + 1]
        rows = lax.broadcasted_iota(jnp.int32, (n - low, 1), 0) + low
        part = a_ref[low:, :]
        f = jnp.where(rows > j, part[:, j:j + 1] * inv, 0.0)
        a_ref[low:, :] = part - f * row_a
        e_ref[low:, :] = e_ref[low:, :] - f * e_ref[j:j + 1, :]
    diag = jnp.where(eye, a_ref[...], 0.0)
    return jnp.sum(diag, axis=1, keepdims=True), jnp.sum(diag, axis=0, keepdims=True)


def _iterate_kernel(g_ref, s_ref, o_ref, a0_ref, e0_ref, a1_ref, e1_ref):
    o_ref[...] = s_ref[...]

    def step(i, carry):
        product = _mm(o_ref[...], g_ref[...])
        moment = _mm_nt(product, product)
        a0_ref[...] = moment[0:HALF, 0:HALF]
        d0c, d0r = _eliminate(a0_ref, e0_ref)
        e0 = e0_ref[...]
        c = _mm_nt(moment[HALF:, 0:HALF], e0) / d0r
        a1_ref[...] = moment[HALF:, HALF:] - _mm_nt(c * d0r, c)
        d1c, _ = _eliminate(a1_ref, e1_ref)
        q0 = _mm(e0, product[0:HALF, :])
        q1 = _mm(e1_ref[...], product[HALF:, :] - _mm(c, q0))
        o_ref[0:HALF, :] = q0 * lax.rsqrt(d0c)
        o_ref[HALF:, :] = q1 * lax.rsqrt(d1c)
        return carry

    lax.fori_loop(0, ITERS, step, 0)


def iterate(gram, start):
    rank = start.shape[0]
    rest = rank - HALF
    return pl.pallas_call(
        _iterate_kernel,
        out_shape=jax.ShapeDtypeStruct(start.shape, jnp.float32),
        scratch_shapes=[
            pltpu.VMEM((HALF, HALF), jnp.float32),
            pltpu.VMEM((HALF, HALF), jnp.float32),
            pltpu.VMEM((rest, rest), jnp.float32),
            pltpu.VMEM((rest, rest), jnp.float32),
        ],
    )(gram, start)


def local(prefill_keys, queries, outlier_spans, start_basis):
    rows_dev = prefill_keys.shape[0]
    width = prefill_keys.shape[1]
    inverse_tokens = 1.0 / (rows_dev * lax.axis_size("kv") * lax.axis_size("seq"))
    scale_factor = 1.0 / math.sqrt(HEAD)
    spanned = prefill_keys.reshape(rows_dev // SPAN, SPAN, width)
    landmarks = jnp.mean(spanned, axis=1, dtype=jnp.float32).astype(jnp.bfloat16)
    picked = jnp.take(spanned, outlier_spans, axis=0).reshape(-1, width)
    query_count = queries.shape[0]
    query_heads = jnp.transpose(queries.reshape(query_count, KVH, GROUP, HEAD), (1, 0, 2, 3))

    def score_rows(shard_rows):
        count_rows = shard_rows.shape[0]
        key_heads = jnp.swapaxes(shard_rows.reshape(count_rows, KVH, HEAD), 0, 1)

        def one_head(pairing):
            query_group, key_group = pairing
            scores = jnp.einsum(
                "qgd,cd->qgc", query_group, key_group, preferred_element_type=jnp.float32
            )
            return jnp.max(scores, axis=1)

        return (lax.map(one_head, (query_heads, key_heads)) * scale_factor).astype(jnp.bfloat16)

    landmark_scores = score_rows(lax.all_gather(landmarks, "seq", axis=0, tiled=True))
    outlier_scores = score_rows(lax.all_gather(picked, "seq", axis=0, tiled=True))
    gram = lax.psum(
        lax.dot_general(
            prefill_keys, prefill_keys, (((0,), (0,)), ((), ())), preferred_element_type=jnp.float32
        ),
        ("kv", "seq"),
    ) * inverse_tokens
    subspace = iterate(gram, start_basis)
    rounded = subspace.astype(jnp.bfloat16)
    coefficients = lax.dot_general(
        rounded, prefill_keys, (((1,), (1,)), ((), ())), preferred_element_type=jnp.float32
    ).astype(jnp.bfloat16)
    return (subspace, coefficients, landmark_scores, outlier_scores)


def solution(mesh):
    placed = (P(("kv", "seq"), None), P("seq", None), P(("kv", "seq")), P())
    return jax.shard_map(
        local,
        mesh=mesh,
        in_specs=placed,
        out_specs=(P(), P(None, ("kv", "seq")), P(None, "seq", "kv"), P(None, "seq", "kv")),
        check_vma=False,
    )
```

```python
import math

import jax
import jax.numpy as jnp
from jax import lax
from jax.experimental import pallas as pl
from jax.experimental.pallas import tpu as pltpu
from jax.sharding import PartitionSpec as P

HI = lax.Precision.HIGHEST
HALF = 128

KVH = 8
HEAD = 128
GROUP = 8
ITERS = 8
SPAN = 8


def _mm(a, b):
    return jnp.dot(a, b, precision=HI, preferred_element_type=jnp.float32)


def _mm_nt(a, b):
    return lax.dot_general(
        a, b, (((1,), (1,)), ((), ())), precision=HI, preferred_element_type=jnp.float32
    )


def _eliminate(a_ref, e_ref):
    n = a_ref.shape[0]
    eye = lax.broadcasted_iota(jnp.int32, (n, n), 0) == lax.broadcasted_iota(jnp.int32, (n, n), 1)
    e_ref[...] = eye.astype(jnp.float32)
    for j in range(n):
        low = (j // 8) * 8
        row_a = a_ref[j:j + 1, :]
        inv = 1.0 / row_a[:, j:j + 1]
        rows = lax.broadcasted_iota(jnp.int32, (n - low, 1), 0) + low
        part = a_ref[low:, :]
        f = jnp.where(rows > j, part[:, j:j + 1] * inv, 0.0)
        a_ref[low:, :] = part - f * row_a
        e_ref[low:, :] = e_ref[low:, :] - f * e_ref[j:j + 1, :]
    diag = jnp.where(eye, a_ref[...], 0.0)
    return jnp.sum(diag, axis=1, keepdims=True), jnp.sum(diag, axis=0, keepdims=True)


def _iterate_kernel(g_ref, s_ref, o_ref, a0_ref, e0_ref, a1_ref, e1_ref):
    o_ref[...] = s_ref[...]

    def step(i, carry):
        product = _mm(o_ref[...], g_ref[...])
        moment = _mm_nt(product, product)
        a0_ref[...] = moment[0:HALF, 0:HALF]
        d0c, d0r = _eliminate(a0_ref, e0_ref)
        e0 = e0_ref[...]
        c = _mm_nt(moment[HALF:, 0:HALF], e0) / d0r
        a1_ref[...] = moment[HALF:, HALF:] - _mm_nt(c * d0r, c)
        d1c, _ = _eliminate(a1_ref, e1_ref)
        q0 = _mm(e0, product[0:HALF, :])
        q1 = _mm(e1_ref[...], product[HALF:, :] - _mm(c, q0))
        o_ref[0:HALF, :] = q0 * lax.rsqrt(d0c)
        o_ref[HALF:, :] = q1 * lax.rsqrt(d1c)
        return carry

    lax.fori_loop(0, ITERS, step, 0)


def iterate(gram, start):
    rank = start.shape[0]
    rest = rank - HALF
    return pl.pallas_call(
        _iterate_kernel,
        out_shape=jax.ShapeDtypeStruct(start.shape, jnp.float32),
        scratch_shapes=[
            pltpu.VMEM((HALF, HALF), jnp.float32),
            pltpu.VMEM((HALF, HALF), jnp.float32),
            pltpu.VMEM((rest, rest), jnp.float32),
            pltpu.VMEM((rest, rest), jnp.float32),
        ],
    )(gram, start)


def _swap(x, flip):
    return lax.ppermute(x, "seq", [(i, i ^ flip) for i in range(lax.axis_size("seq"))])


def _halve(x, bit, flip):
    rows = x.shape[0] // 2
    keep = lax.dynamic_slice_in_dim(x, bit * rows, rows)
    send = lax.dynamic_slice_in_dim(x, (1 - bit) * rows, rows)
    return keep + _swap(send, flip)


def _double(x, bit, flip):
    other = _swap(x, flip)
    rows = x.shape[0]
    out = jnp.zeros((2 * rows,) + x.shape[1:], x.dtype)
    out = lax.dynamic_update_slice_in_dim(out, x, bit * rows, 0)
    return lax.dynamic_update_slice_in_dim(out, other, (1 - bit) * rows, 0)


def sum_gram(local_gram):
    seq = lax.axis_index("seq")
    kv_size = lax.axis_size("kv")
    core, z_low, z_high = seq % 2, (seq // 2) % 2, (seq // 4) % 2
    s = _halve(local_gram, core, 1)
    s = lax.all_to_all(s.reshape((kv_size, -1) + s.shape[1:]), "kv", 0, 0, tiled=True)
    s = jnp.sum(s, axis=0)
    s = _halve(_halve(s, z_high, 4), z_low, 2)
    s = _double(_double(s, z_low, 2), z_high, 4)
    s = lax.all_gather(s, "kv", axis=0, tiled=True)
    return _double(s, core, 1)


def local(prefill_keys, queries, outlier_spans, start_basis):
    rows_dev = prefill_keys.shape[0]
    width = prefill_keys.shape[1]
    inverse_tokens = 1.0 / (rows_dev * lax.axis_size("kv") * lax.axis_size("seq"))
    scale_factor = 1.0 / math.sqrt(HEAD)
    spanned = prefill_keys.reshape(rows_dev // SPAN, SPAN, width)
    landmarks = jnp.mean(spanned, axis=1, dtype=jnp.float32).astype(jnp.bfloat16)
    picked = jnp.take(spanned, outlier_spans, axis=0).reshape(-1, width)
    query_count = queries.shape[0]
    query_heads = jnp.transpose(queries.reshape(query_count, KVH, GROUP, HEAD), (1, 0, 2, 3))

    def score_rows(shard_rows):
        count_rows = shard_rows.shape[0]
        key_heads = jnp.swapaxes(shard_rows.reshape(count_rows, KVH, HEAD), 0, 1)

        def one_head(pairing):
            query_group, key_group = pairing
            scores = jnp.einsum(
                "qgd,cd->qgc", query_group, key_group, preferred_element_type=jnp.float32
            )
            return jnp.max(scores, axis=1)

        return (lax.map(one_head, (query_heads, key_heads)) * scale_factor).astype(jnp.bfloat16)

    landmark_scores = score_rows(lax.all_gather(landmarks, "seq", axis=0, tiled=True))
    outlier_scores = score_rows(lax.all_gather(picked, "seq", axis=0, tiled=True))
    local_gram = lax.dot_general(
        prefill_keys, prefill_keys, (((0,), (0,)), ((), ())), preferred_element_type=jnp.float32
    ) * inverse_tokens
    gram = sum_gram(local_gram)
    subspace = iterate(gram, start_basis)
    rounded = subspace.astype(jnp.bfloat16)
    coefficients = lax.dot_general(
        rounded, prefill_keys, (((1,), (1,)), ((), ())), preferred_element_type=jnp.float32
    ).astype(jnp.bfloat16)
    return (subspace, coefficients, landmark_scores, outlier_scores)


def solution(mesh):
    placed = (P(("kv", "seq"), None), P("seq", None), P(("kv", "seq")), P())
    return jax.shard_map(
        local,
        mesh=mesh,
        in_specs=placed,
        out_specs=(P(), P(None, ("kv", "seq")), P(None, "seq", "kv"), P(None, "seq", "kv")),
        check_vma=False,
    )
```

```python
import math

import jax
import jax.numpy as jnp
from jax import lax
from jax.experimental import pallas as pl
from jax.experimental.pallas import tpu as pltpu
from jax.sharding import PartitionSpec as P

HI = lax.Precision.HIGHEST
HALF = 128

KVH = 8
HEAD = 128
GROUP = 8
ITERS = 8
SPAN = 8


def _mm(a, b):
    return jnp.dot(a, b, precision=HI, preferred_element_type=jnp.float32)


def _mm_nt(a, b):
    return lax.dot_general(
        a, b, (((1,), (1,)), ((), ())), precision=HI, preferred_element_type=jnp.float32
    )


def _eliminate(a_ref, e_ref):
    n = a_ref.shape[0]
    eye = lax.broadcasted_iota(jnp.int32, (n, n), 0) == lax.broadcasted_iota(jnp.int32, (n, n), 1)
    e_ref[...] = eye.astype(jnp.float32)
    for j in range(n):
        low = (j // 8) * 8
        row_a = a_ref[j:j + 1, :]
        inv = 1.0 / row_a[:, j:j + 1]
        rows = lax.broadcasted_iota(jnp.int32, (n - low, 1), 0) + low
        part = a_ref[low:, :]
        f = jnp.where(rows > j, part[:, j:j + 1] * inv, 0.0)
        a_ref[low:, :] = part - f * row_a
        e_ref[low:, :] = e_ref[low:, :] - f * e_ref[j:j + 1, :]
    diag = jnp.where(eye, a_ref[...], 0.0)
    return jnp.sum(diag, axis=1, keepdims=True), jnp.sum(diag, axis=0, keepdims=True)


def _iterate_kernel(g_ref, s_ref, o_ref, a0_ref, e0_ref, a1_ref, e1_ref):
    o_ref[...] = s_ref[...]

    def step(i, carry):
        product = _mm(o_ref[...], g_ref[...])
        moment = _mm_nt(product, product)
        a0_ref[...] = moment[0:HALF, 0:HALF]
        d0c, d0r = _eliminate(a0_ref, e0_ref)
        e0 = e0_ref[...]
        c = _mm_nt(moment[HALF:, 0:HALF], e0) / d0r
        a1_ref[...] = moment[HALF:, HALF:] - _mm_nt(c * d0r, c)
        d1c, _ = _eliminate(a1_ref, e1_ref)
        q0 = _mm(e0, product[0:HALF, :])
        q1 = _mm(e1_ref[...], product[HALF:, :] - _mm(c, q0))
        o_ref[0:HALF, :] = q0 * lax.rsqrt(d0c)
        o_ref[HALF:, :] = q1 * lax.rsqrt(d1c)
        return carry

    lax.fori_loop(0, ITERS, step, 0)


def iterate(gram, start):
    rank = start.shape[0]
    rest = rank - HALF
    return pl.pallas_call(
        _iterate_kernel,
        out_shape=jax.ShapeDtypeStruct(start.shape, jnp.float32),
        scratch_shapes=[
            pltpu.VMEM((HALF, HALF), jnp.float32),
            pltpu.VMEM((HALF, HALF), jnp.float32),
            pltpu.VMEM((rest, rest), jnp.float32),
            pltpu.VMEM((rest, rest), jnp.float32),
        ],
    )(gram, start)


def _swap(x, flip, axis="seq"):
    return lax.ppermute(x, axis, [(i, i ^ flip) for i in range(lax.axis_size(axis))])


def _halve(x, bit, flip):
    rows = x.shape[0] // 2
    keep = lax.dynamic_slice_in_dim(x, bit * rows, rows)
    send = lax.dynamic_slice_in_dim(x, (1 - bit) * rows, rows)
    return keep + _swap(send, flip)


def _double(x, bit, flip, axis="seq"):
    other = _swap(x, flip, axis)
    rows = x.shape[0]
    out = jnp.zeros((2 * rows,) + x.shape[1:], x.dtype)
    out = lax.dynamic_update_slice_in_dim(out, x, bit * rows, 0)
    return lax.dynamic_update_slice_in_dim(out, other, (1 - bit) * rows, 0)


def sum_gram(local_gram, early, late):
    seq = lax.axis_index("seq")
    kv = lax.axis_index("kv")
    kv_size = lax.axis_size("kv")
    core, z_low, z_high = seq % 2, (seq // 2) % 2, (seq // 4) % 2
    s = _halve(local_gram, core, 1)
    s = lax.all_to_all(s.reshape((kv_size, -1) + s.shape[1:]), "kv", 0, 0, tiled=True)
    s, early = lax.optimization_barrier((s, early))
    s = jnp.sum(s, axis=0)
    s = _halve(_halve(s, z_high, 4), z_low, 2)
    s = _double(_double(s, z_low, 2), z_high, 4)
    flip = 1
    while flip < kv_size:
        s = _double(s, (kv // flip) % 2, flip, "kv")
        flip *= 2
    s, late = lax.optimization_barrier((s, late))
    return _double(s, core, 1), early, late


def local(prefill_keys, queries, outlier_spans, start_basis):
    rows_dev = prefill_keys.shape[0]
    width = prefill_keys.shape[1]
    inverse_tokens = 1.0 / (rows_dev * lax.axis_size("kv") * lax.axis_size("seq"))
    scale_factor = 1.0 / math.sqrt(HEAD)
    spanned = prefill_keys.reshape(rows_dev // SPAN, SPAN, width)
    landmarks = jnp.mean(spanned, axis=1, dtype=jnp.float32).astype(jnp.bfloat16)
    picked = jnp.take(spanned, outlier_spans, axis=0).reshape(-1, width)
    query_count = queries.shape[0]
    query_heads = jnp.transpose(queries.reshape(query_count, KVH, GROUP, HEAD), (1, 0, 2, 3))

    def score_rows(shard_rows):
        count_rows = shard_rows.shape[0]
        key_heads = jnp.swapaxes(shard_rows.reshape(count_rows, KVH, HEAD), 0, 1)

        def one_head(pairing):
            query_group, key_group = pairing
            scores = jnp.einsum(
                "qgd,cd->qgc", query_group, key_group, preferred_element_type=jnp.float32
            )
            return jnp.max(scores, axis=1)

        return (lax.map(one_head, (query_heads, key_heads)) * scale_factor).astype(jnp.bfloat16)

    landmark_scores = score_rows(lax.all_gather(landmarks, "seq", axis=0, tiled=True))
    outlier_scores = score_rows(lax.all_gather(picked, "seq", axis=0, tiled=True))
    local_gram = lax.dot_general(
        prefill_keys, prefill_keys, (((0,), (0,)), ((), ())), preferred_element_type=jnp.float32
    ) * inverse_tokens
    gram, outlier_scores, landmark_scores = sum_gram(local_gram, outlier_scores, landmark_scores)
    subspace = iterate(gram, start_basis)
    rounded = subspace.astype(jnp.bfloat16)
    coefficients = lax.dot_general(
        rounded, prefill_keys, (((1,), (1,)), ((), ())), preferred_element_type=jnp.float32
    ).astype(jnp.bfloat16)
    return (subspace, coefficients, landmark_scores, outlier_scores)


def solution(mesh):
    placed = (P(("kv", "seq"), None), P("seq", None), P(("kv", "seq")), P())
    return jax.shard_map(
        local,
        mesh=mesh,
        in_specs=placed,
        out_specs=(P(), P(None, ("kv", "seq")), P(None, "seq", "kv"), P(None, "seq", "kv")),
        check_vma=False,
    )
```

```python
import math

import jax
import jax.numpy as jnp
from jax import lax
from jax.experimental import pallas as pl
from jax.experimental.pallas import tpu as pltpu
from jax.sharding import PartitionSpec as P

HI = lax.Precision.HIGHEST
HALF = 128

KVH = 8
HEAD = 128
GROUP = 8
ITERS = 8
SPAN = 8


def _mm(a, b):
    return jnp.dot(a, b, precision=HI, preferred_element_type=jnp.float32)


def _mm_nt(a, b):
    return lax.dot_general(
        a, b, (((1,), (1,)), ((), ())), precision=HI, preferred_element_type=jnp.float32
    )


def _eliminate(a_ref, e_ref):
    n = a_ref.shape[0]
    eye = lax.broadcasted_iota(jnp.int32, (n, n), 0) == lax.broadcasted_iota(jnp.int32, (n, n), 1)
    e_ref[...] = eye.astype(jnp.float32)
    for j in range(n):
        low = (j // 8) * 8
        row_a = a_ref[j:j + 1, :]
        inv = 1.0 / row_a[:, j:j + 1]
        rows = lax.broadcasted_iota(jnp.int32, (n - low, 1), 0) + low
        part = a_ref[low:, :]
        f = jnp.where(rows > j, part[:, j:j + 1] * inv, 0.0)
        a_ref[low:, :] = part - f * row_a
        e_ref[low:, :] = e_ref[low:, :] - f * e_ref[j:j + 1, :]
    diag = jnp.where(eye, a_ref[...], 0.0)
    return jnp.sum(diag, axis=1, keepdims=True), jnp.sum(diag, axis=0, keepdims=True)


def _iterate_kernel(g_ref, s_ref, o_ref, a0_ref, e0_ref, a1_ref, e1_ref):
    o_ref[...] = s_ref[...]

    def step(i, carry):
        product = _mm(o_ref[...], g_ref[...])
        moment = _mm_nt(product, product)
        a0_ref[...] = moment[0:HALF, 0:HALF]
        d0c, d0r = _eliminate(a0_ref, e0_ref)
        e0 = e0_ref[...]
        c = _mm_nt(moment[HALF:, 0:HALF], e0) / d0r
        a1_ref[...] = moment[HALF:, HALF:] - _mm_nt(c * d0r, c)
        d1c, _ = _eliminate(a1_ref, e1_ref)
        q0 = _mm(e0, product[0:HALF, :])
        q1 = _mm(e1_ref[...], product[HALF:, :] - _mm(c, q0))
        o_ref[0:HALF, :] = q0 * lax.rsqrt(d0c)
        o_ref[HALF:, :] = q1 * lax.rsqrt(d1c)
        return carry

    lax.fori_loop(0, ITERS, step, 0)


def iterate(gram, start):
    rank = start.shape[0]
    rest = rank - HALF
    return pl.pallas_call(
        _iterate_kernel,
        out_shape=jax.ShapeDtypeStruct(start.shape, jnp.float32),
        scratch_shapes=[
            pltpu.VMEM((HALF, HALF), jnp.float32),
            pltpu.VMEM((HALF, HALF), jnp.float32),
            pltpu.VMEM((rest, rest), jnp.float32),
            pltpu.VMEM((rest, rest), jnp.float32),
        ],
    )(gram, start)


def _swap(x, flip, axis="seq"):
    return lax.ppermute(x, axis, [(i, i ^ flip) for i in range(lax.axis_size(axis))])


def _halve(x, bit, flip):
    rows = x.shape[0] // 2
    keep = lax.dynamic_slice_in_dim(x, bit * rows, rows)
    send = lax.dynamic_slice_in_dim(x, (1 - bit) * rows, rows)
    return keep + _swap(send, flip)


def _double(x, bit, flip, axis="seq"):
    other = _swap(x, flip, axis)
    rows = x.shape[0]
    out = jnp.zeros((2 * rows,) + x.shape[1:], x.dtype)
    out = lax.dynamic_update_slice_in_dim(out, x, bit * rows, 0)
    return lax.dynamic_update_slice_in_dim(out, other, (1 - bit) * rows, 0)


def sum_gram(local_gram, early, late):
    seq = lax.axis_index("seq")
    kv_size = lax.axis_size("kv")
    core, z_low, z_high = seq % 2, (seq // 2) % 2, (seq // 4) % 2
    s = _halve(local_gram, core, 1)
    s = lax.all_to_all(s.reshape((kv_size, -1) + s.shape[1:]), "kv", 0, 0, tiled=True)
    s, early = lax.optimization_barrier((s, early))
    s = jnp.sum(s, axis=0)
    s = _halve(_halve(s, z_high, 4), z_low, 2)
    s = _double(_double(s, z_low, 2), z_high, 4)
    s = lax.all_gather(s, "kv", axis=0, tiled=True)
    s, late = lax.optimization_barrier((s, late))
    return _double(s, core, 1), early, late


def local(prefill_keys, queries, outlier_spans, start_basis):
    rows_dev = prefill_keys.shape[0]
    width = prefill_keys.shape[1]
    inverse_tokens = 1.0 / (rows_dev * lax.axis_size("kv") * lax.axis_size("seq"))
    scale_factor = 1.0 / math.sqrt(HEAD)
    spanned = prefill_keys.reshape(rows_dev // SPAN, SPAN, width)
    landmarks = jnp.mean(spanned, axis=1, dtype=jnp.float32).astype(jnp.bfloat16)
    picked = jnp.take(spanned, outlier_spans, axis=0).reshape(-1, width)
    query_count = queries.shape[0]
    query_heads = jnp.transpose(queries.reshape(query_count, KVH, GROUP, HEAD), (1, 0, 2, 3))

    def score_rows(shard_rows):
        count_rows = shard_rows.shape[0]
        key_heads = jnp.swapaxes(shard_rows.reshape(count_rows, KVH, HEAD), 0, 1)

        def one_head(pairing):
            query_group, key_group = pairing
            scores = jnp.einsum(
                "qgd,cd->qgc", query_group, key_group, preferred_element_type=jnp.float32
            )
            return jnp.max(scores, axis=1)

        return (lax.map(one_head, (query_heads, key_heads)) * scale_factor).astype(jnp.bfloat16)

    landmark_scores = score_rows(lax.all_gather(landmarks, "seq", axis=0, tiled=True))
    outlier_scores = score_rows(lax.all_gather(picked, "seq", axis=0, tiled=True))
    local_gram = lax.dot_general(
        prefill_keys, prefill_keys, (((0,), (0,)), ((), ())), preferred_element_type=jnp.float32
    ) * inverse_tokens
    gram, landmark_scores, outlier_scores = sum_gram(local_gram, landmark_scores, outlier_scores)
    subspace = iterate(gram, start_basis)
    rounded = subspace.astype(jnp.bfloat16)
    coefficients = lax.dot_general(
        rounded, prefill_keys, (((1,), (1,)), ((), ())), preferred_element_type=jnp.float32
    ).astype(jnp.bfloat16)
    return (subspace, coefficients, landmark_scores, outlier_scores)


def solution(mesh):
    placed = (P(("kv", "seq"), None), P("seq", None), P(("kv", "seq")), P())
    return jax.shard_map(
        local,
        mesh=mesh,
        in_specs=placed,
        out_specs=(P(), P(None, ("kv", "seq")), P(None, "seq", "kv"), P(None, "seq", "kv")),
        check_vma=False,
    )
```

```python
import math

import jax
import jax.numpy as jnp
from jax import lax
from jax.experimental import pallas as pl
from jax.experimental.pallas import tpu as pltpu
from jax.sharding import PartitionSpec as P

HI = lax.Precision.HIGHEST
HALF = 128

KVH = 8
HEAD = 128
GROUP = 8
ITERS = 8
SPAN = 8


def _mm(a, b):
    return jnp.dot(a, b, precision=HI, preferred_element_type=jnp.float32)


def _mm_nt(a, b):
    return lax.dot_general(
        a, b, (((1,), (1,)), ((), ())), precision=HI, preferred_element_type=jnp.float32
    )


def _eliminate(a_ref, e_ref):
    n = a_ref.shape[0]
    eye = lax.broadcasted_iota(jnp.int32, (n, n), 0) == lax.broadcasted_iota(jnp.int32, (n, n), 1)
    e_ref[...] = eye.astype(jnp.float32)
    for j in range(n):
        low = (j // 8) * 8
        row_a = a_ref[j:j + 1, :]
        inv = 1.0 / row_a[:, j:j + 1]
        rows = lax.broadcasted_iota(jnp.int32, (n - low, 1), 0) + low
        part = a_ref[low:, :]
        f = jnp.where(rows > j, part[:, j:j + 1] * inv, 0.0)
        a_ref[low:, :] = part - f * row_a
        e_ref[low:, :] = e_ref[low:, :] - f * e_ref[j:j + 1, :]
    diag = jnp.where(eye, a_ref[...], 0.0)
    return jnp.sum(diag, axis=1, keepdims=True), jnp.sum(diag, axis=0, keepdims=True)


def _iterate_kernel(g_ref, s_ref, o_ref, a0_ref, e0_ref, a1_ref, e1_ref):
    o_ref[...] = s_ref[...]

    def step(i, carry):
        product = _mm(o_ref[...], g_ref[...])
        moment = _mm_nt(product, product)
        a0_ref[...] = moment[0:HALF, 0:HALF]
        d0c, d0r = _eliminate(a0_ref, e0_ref)
        e0 = e0_ref[...]
        c = _mm_nt(moment[HALF:, 0:HALF], e0) / d0r
        a1_ref[...] = moment[HALF:, HALF:] - _mm_nt(c * d0r, c)
        d1c, _ = _eliminate(a1_ref, e1_ref)
        q0 = _mm(e0, product[0:HALF, :])
        q1 = _mm(e1_ref[...], product[HALF:, :] - _mm(c, q0))
        o_ref[0:HALF, :] = q0 * lax.rsqrt(d0c)
        o_ref[HALF:, :] = q1 * lax.rsqrt(d1c)
        return carry

    lax.fori_loop(0, ITERS, step, 0)


def iterate(gram, start):
    rank = start.shape[0]
    rest = rank - HALF
    return pl.pallas_call(
        _iterate_kernel,
        out_shape=jax.ShapeDtypeStruct(start.shape, jnp.float32),
        scratch_shapes=[
            pltpu.VMEM((HALF, HALF), jnp.float32),
            pltpu.VMEM((HALF, HALF), jnp.float32),
            pltpu.VMEM((rest, rest), jnp.float32),
            pltpu.VMEM((rest, rest), jnp.float32),
        ],
    )(gram, start)


def _swap(x, flip, axis="seq"):
    return lax.ppermute(x, axis, [(i, i ^ flip) for i in range(lax.axis_size(axis))])


def _halve(x, bit, flip):
    rows = x.shape[0] // 2
    keep = lax.dynamic_slice_in_dim(x, bit * rows, rows)
    send = lax.dynamic_slice_in_dim(x, (1 - bit) * rows, rows)
    return keep + _swap(send, flip)


def _double(x, bit, flip, axis="seq"):
    other = _swap(x, flip, axis)
    rows = x.shape[0]
    out = jnp.zeros((2 * rows,) + x.shape[1:], x.dtype)
    out = lax.dynamic_update_slice_in_dim(out, x, bit * rows, 0)
    return lax.dynamic_update_slice_in_dim(out, other, (1 - bit) * rows, 0)


def sum_gram(local_gram, early, late):
    seq = lax.axis_index("seq")
    kv_size = lax.axis_size("kv")
    core, z_low, z_high = seq % 2, (seq // 2) % 2, (seq // 4) % 2
    s = _halve(local_gram, core, 1)
    s = lax.all_to_all(s.reshape((kv_size, -1) + s.shape[1:]), "kv", 0, 0, tiled=True)
    s, early = lax.optimization_barrier((s, early))
    s = jnp.sum(s, axis=0)
    s = _halve(_halve(s, z_high, 4), z_low, 2)
    s = _double(_double(s, z_low, 2), z_high, 4)
    s = lax.all_gather(s, "kv", axis=0, tiled=True)
    s, late = lax.optimization_barrier((s, late))
    return _double(s, core, 1), early, late


def local(prefill_keys, queries, outlier_spans, start_basis):
    rows_dev = prefill_keys.shape[0]
    width = prefill_keys.shape[1]
    inverse_tokens = 1.0 / (rows_dev * lax.axis_size("kv") * lax.axis_size("seq"))
    scale_factor = 1.0 / math.sqrt(HEAD)
    spanned = prefill_keys.reshape(rows_dev // SPAN, SPAN, width)
    landmarks = jnp.mean(spanned, axis=1, dtype=jnp.float32).astype(jnp.bfloat16)
    picked = jnp.take(spanned, outlier_spans, axis=0).reshape(-1, width)
    query_count = queries.shape[0]
    query_heads = jnp.transpose(queries.reshape(query_count, KVH, GROUP, HEAD), (1, 0, 2, 3))

    def score_rows(shard_rows):
        count_rows = shard_rows.shape[0]
        key_heads = jnp.swapaxes(shard_rows.reshape(count_rows, KVH, HEAD), 0, 1)

        def one_head(pairing):
            query_group, key_group = pairing
            scores = jnp.einsum(
                "qgd,cd->qgc", query_group, key_group, preferred_element_type=jnp.float32
            )
            return (jnp.max(scores, axis=1) * scale_factor).astype(jnp.bfloat16)

        return lax.map(one_head, (query_heads, key_heads))

    landmark_scores = score_rows(lax.all_gather(landmarks, "seq", axis=0, tiled=True))
    outlier_scores = score_rows(lax.all_gather(picked, "seq", axis=0, tiled=True))
    local_gram = lax.dot_general(
        prefill_keys, prefill_keys, (((0,), (0,)), ((), ())), preferred_element_type=jnp.float32
    ) * inverse_tokens
    gram, landmark_scores, outlier_scores = sum_gram(local_gram, landmark_scores, outlier_scores)
    subspace = iterate(gram, start_basis)
    rounded = subspace.astype(jnp.bfloat16)
    coefficients = lax.dot_general(
        rounded, prefill_keys, (((1,), (1,)), ((), ())), preferred_element_type=jnp.float32
    ).astype(jnp.bfloat16)
    return (subspace, coefficients, landmark_scores, outlier_scores)


def solution(mesh):
    placed = (P(("kv", "seq"), None), P("seq", None), P(("kv", "seq")), P())
    return jax.shard_map(
        local,
        mesh=mesh,
        in_specs=placed,
        out_specs=(P(), P(None, ("kv", "seq")), P(None, "seq", "kv"), P(None, "seq", "kv")),
        check_vma=False,
    )
```

```python
import math

import jax
import jax.numpy as jnp
from jax import lax
from jax.experimental import pallas as pl
from jax.experimental.pallas import tpu as pltpu
from jax.sharding import PartitionSpec as P

HI = lax.Precision.HIGHEST
HALF = 128

KVH = 8
HEAD = 128
GROUP = 8
ITERS = 8
SPAN = 8


def _mm(a, b):
    return jnp.dot(a, b, precision=HI, preferred_element_type=jnp.float32)


def _mm_nt(a, b):
    return lax.dot_general(
        a, b, (((1,), (1,)), ((), ())), precision=HI, preferred_element_type=jnp.float32
    )


def _eliminate(a_ref, e_ref):
    n = a_ref.shape[0]
    eye = lax.broadcasted_iota(jnp.int32, (n, n), 0) == lax.broadcasted_iota(jnp.int32, (n, n), 1)
    e_ref[...] = eye.astype(jnp.float32)
    for j in range(n):
        low = (j // 8) * 8
        row_a = a_ref[j:j + 1, :]
        inv = 1.0 / row_a[:, j:j + 1]
        rows = lax.broadcasted_iota(jnp.int32, (n - low, 1), 0) + low
        part = a_ref[low:, :]
        f = jnp.where(rows > j, part[:, j:j + 1] * inv, 0.0)
        a_ref[low:, :] = part - f * row_a
        e_ref[low:, :] = e_ref[low:, :] - f * e_ref[j:j + 1, :]
    diag = jnp.where(eye, a_ref[...], 0.0)
    return jnp.sum(diag, axis=1, keepdims=True), jnp.sum(diag, axis=0, keepdims=True)


def _iterate_kernel(low_ref, mine_ref, other_ref, s_ref, o_ref, a0_ref, e0_ref, a1_ref, e1_ref):
    o_ref[...] = s_ref[...]
    width = mine_ref.shape[0]
    low = low_ref[...] > 0.5

    def step(i, carry):
        subspace = o_ref[...]
        first = subspace[:, 0:width]
        second = subspace[:, width:]
        product = _mm(jnp.where(low, first, second), mine_ref[...]) + _mm(
            jnp.where(low, second, first), other_ref[...]
        )
        moment = _mm_nt(product, product)
        a0_ref[...] = moment[0:HALF, 0:HALF]
        d0c, d0r = _eliminate(a0_ref, e0_ref)
        e0 = e0_ref[...]
        c = _mm_nt(moment[HALF:, 0:HALF], e0) / d0r
        a1_ref[...] = moment[HALF:, HALF:] - _mm_nt(c * d0r, c)
        d1c, _ = _eliminate(a1_ref, e1_ref)
        q0 = _mm(e0, product[0:HALF, :])
        q1 = _mm(e1_ref[...], product[HALF:, :] - _mm(c, q0))
        o_ref[0:HALF, :] = q0 * lax.rsqrt(d0c)
        o_ref[HALF:, :] = q1 * lax.rsqrt(d1c)
        return carry

    lax.fori_loop(0, ITERS, step, 0)


def iterate(low, mine, other, start):
    rank = start.shape[0]
    rest = rank - HALF
    return pl.pallas_call(
        _iterate_kernel,
        out_shape=jax.ShapeDtypeStruct(start.shape, jnp.float32),
        scratch_shapes=[
            pltpu.VMEM((HALF, HALF), jnp.float32),
            pltpu.VMEM((HALF, HALF), jnp.float32),
            pltpu.VMEM((rest, rest), jnp.float32),
            pltpu.VMEM((rest, rest), jnp.float32),
        ],
    )(low, mine, other, start)


def _swap(x, flip, axis="seq"):
    return lax.ppermute(x, axis, [(i, i ^ flip) for i in range(lax.axis_size(axis))])


def _halve(x, bit, flip):
    rows = x.shape[0] // 2
    keep = lax.dynamic_slice_in_dim(x, bit * rows, rows)
    send = lax.dynamic_slice_in_dim(x, (1 - bit) * rows, rows)
    return keep + _swap(send, flip)


def _double(x, bit, flip, axis="seq"):
    other = _swap(x, flip, axis)
    rows = x.shape[0]
    out = jnp.zeros((2 * rows,) + x.shape[1:], x.dtype)
    out = lax.dynamic_update_slice_in_dim(out, x, bit * rows, 0)
    return lax.dynamic_update_slice_in_dim(out, other, (1 - bit) * rows, 0)


def sum_gram(local_gram, early, late):
    seq = lax.axis_index("seq")
    kv_size = lax.axis_size("kv")
    core, z_low, z_high = seq % 2, (seq // 2) % 2, (seq // 4) % 2
    s = _halve(local_gram, core, 1)
    s = lax.all_to_all(s.reshape((kv_size, -1) + s.shape[1:]), "kv", 0, 0, tiled=True)
    s, early = lax.optimization_barrier((s, early))
    s = jnp.sum(s, axis=0)
    s = _halve(_halve(s, z_high, 4), z_low, 2)
    s = _double(_double(s, z_low, 2), z_high, 4)
    s = lax.all_gather(s, "kv", axis=0, tiled=True)
    s, late = lax.optimization_barrier((s, late))
    low = jnp.where(core == 0, 1.0, 0.0).astype(jnp.float32).reshape(1, 1)
    return (low, s, _swap(s, 1)), early, late


def local(prefill_keys, queries, outlier_spans, start_basis):
    rows_dev = prefill_keys.shape[0]
    width = prefill_keys.shape[1]
    inverse_tokens = 1.0 / (rows_dev * lax.axis_size("kv") * lax.axis_size("seq"))
    scale_factor = 1.0 / math.sqrt(HEAD)
    spanned = prefill_keys.reshape(rows_dev // SPAN, SPAN, width)
    landmarks = jnp.mean(spanned, axis=1, dtype=jnp.float32).astype(jnp.bfloat16)
    picked = jnp.take(spanned, outlier_spans, axis=0).reshape(-1, width)
    query_count = queries.shape[0]
    query_heads = jnp.transpose(queries.reshape(query_count, KVH, GROUP, HEAD), (1, 0, 2, 3))

    def score_rows(shard_rows):
        count_rows = shard_rows.shape[0]
        key_heads = jnp.swapaxes(shard_rows.reshape(count_rows, KVH, HEAD), 0, 1)

        def one_head(pairing):
            query_group, key_group = pairing
            scores = jnp.einsum(
                "qgd,cd->qgc", query_group, key_group, preferred_element_type=jnp.float32
            )
            return (jnp.max(scores, axis=1) * scale_factor).astype(jnp.bfloat16)

        return lax.map(one_head, (query_heads, key_heads))

    landmark_scores = score_rows(lax.all_gather(landmarks, "seq", axis=0, tiled=True))
    outlier_scores = score_rows(lax.all_gather(picked, "seq", axis=0, tiled=True))
    local_gram = lax.dot_general(
        prefill_keys, prefill_keys, (((0,), (0,)), ((), ())), preferred_element_type=jnp.float32
    ) * inverse_tokens
    gram, landmark_scores, outlier_scores = sum_gram(local_gram, landmark_scores, outlier_scores)
    subspace = iterate(*gram, start_basis)
    rounded = subspace.astype(jnp.bfloat16)
    coefficients = lax.dot_general(
        rounded, prefill_keys, (((1,), (1,)), ((), ())), preferred_element_type=jnp.float32
    ).astype(jnp.bfloat16)
    return (subspace, coefficients, landmark_scores, outlier_scores)


def solution(mesh):
    placed = (P(("kv", "seq"), None), P("seq", None), P(("kv", "seq")), P())
    return jax.shard_map(
        local,
        mesh=mesh,
        in_specs=placed,
        out_specs=(P(), P(None, ("kv", "seq")), P(None, "seq", "kv"), P(None, "seq", "kv")),
        check_vma=False,
    )
```

```python
import math

import jax
import jax.numpy as jnp
from jax import lax
from jax.experimental import pallas as pl
from jax.experimental.pallas import tpu as pltpu
from jax.sharding import PartitionSpec as P

HI = lax.Precision.HIGHEST
HALF = 128

KVH = 8
HEAD = 128
GROUP = 8
ITERS = 8
SPAN = 8


def _mm(a, b):
    return jnp.dot(a, b, precision=HI, preferred_element_type=jnp.float32)


def _mm_nt(a, b):
    return lax.dot_general(
        a, b, (((1,), (1,)), ((), ())), precision=HI, preferred_element_type=jnp.float32
    )


def _eliminate(a_ref, e_ref):
    n = a_ref.shape[0]
    eye = lax.broadcasted_iota(jnp.int32, (n, n), 0) == lax.broadcasted_iota(jnp.int32, (n, n), 1)
    e_ref[...] = eye.astype(jnp.float32)
    for j in range(n):
        low = (j // 8) * 8
        row_a = a_ref[j:j + 1, :]
        inv = 1.0 / row_a[:, j:j + 1]
        rows = lax.broadcasted_iota(jnp.int32, (n - low, 1), 0) + low
        part = a_ref[low:, :]
        f = jnp.where(rows > j, part[:, j:j + 1] * inv, 0.0)
        a_ref[low:, :] = part - f * row_a
        e_ref[low:, :] = e_ref[low:, :] - f * e_ref[j:j + 1, :]
    diag = jnp.where(eye, a_ref[...], 0.0)
    return jnp.sum(diag, axis=1, keepdims=True), jnp.sum(diag, axis=0, keepdims=True)


def _iterate_kernel(g_ref, s_ref, o_ref, a0_ref, e0_ref, a1_ref, e1_ref):
    o_ref[...] = s_ref[...]

    def step(i, carry):
        product = _mm(o_ref[...], g_ref[...])
        moment = _mm_nt(product, product)
        a0_ref[...] = moment[0:HALF, 0:HALF]
        d0c, d0r = _eliminate(a0_ref, e0_ref)
        e0 = e0_ref[...]
        c = _mm_nt(moment[HALF:, 0:HALF], e0) / d0r
        a1_ref[...] = moment[HALF:, HALF:] - _mm_nt(c * d0r, c)
        d1c, _ = _eliminate(a1_ref, e1_ref)
        q0 = _mm(e0, product[0:HALF, :])
        q1 = _mm(e1_ref[...], product[HALF:, :] - _mm(c, q0))
        o_ref[0:HALF, :] = q0 * lax.rsqrt(d0c)
        o_ref[HALF:, :] = q1 * lax.rsqrt(d1c)
        return carry

    lax.fori_loop(0, ITERS, step, 0)


def iterate(gram, start):
    rank = start.shape[0]
    rest = rank - HALF
    return pl.pallas_call(
        _iterate_kernel,
        out_shape=jax.ShapeDtypeStruct(start.shape, jnp.float32),
        scratch_shapes=[
            pltpu.VMEM((HALF, HALF), jnp.float32),
            pltpu.VMEM((HALF, HALF), jnp.float32),
            pltpu.VMEM((rest, rest), jnp.float32),
            pltpu.VMEM((rest, rest), jnp.float32),
        ],
    )(gram, start)


def _swap(x, flip, axis="seq"):
    return lax.ppermute(x, axis, [(i, i ^ flip) for i in range(lax.axis_size(axis))])


def _halve(x, bit, flip):
    rows = x.shape[0] // 2
    keep = lax.dynamic_slice_in_dim(x, bit * rows, rows)
    send = lax.dynamic_slice_in_dim(x, (1 - bit) * rows, rows)
    return keep + _swap(send, flip)


def _double(x, bit, flip, axis="seq"):
    other = _swap(x, flip, axis)
    rows = x.shape[0]
    out = jnp.zeros((2 * rows,) + x.shape[1:], x.dtype)
    out = lax.dynamic_update_slice_in_dim(out, x, bit * rows, 0)
    return lax.dynamic_update_slice_in_dim(out, other, (1 - bit) * rows, 0)


def sum_gram(local_gram, early, late):
    seq = lax.axis_index("seq")
    kv_size = lax.axis_size("kv")
    core, z_low, z_high = seq % 2, (seq // 2) % 2, (seq // 4) % 2
    s = _halve(local_gram, core, 1)
    s = lax.all_to_all(s.reshape((kv_size, -1) + s.shape[1:]), "kv", 0, 0, tiled=True)
    s, early = lax.optimization_barrier((s, early))
    s = jnp.sum(s, axis=0)
    s = _halve(_halve(s, z_high, 4), z_low, 2)
    s = _double(_double(s, z_low, 2), z_high, 4)
    s = lax.all_gather(s, "kv", axis=0, tiled=True)
    s, late = lax.optimization_barrier((s, late))
    return _double(s, core, 1), early, late


def local(prefill_keys, queries, outlier_spans, start_basis):
    rows_dev = prefill_keys.shape[0]
    width = prefill_keys.shape[1]
    inverse_tokens = 1.0 / (rows_dev * lax.axis_size("kv") * lax.axis_size("seq"))
    scale_factor = 1.0 / math.sqrt(HEAD)
    spanned = prefill_keys.reshape(rows_dev // SPAN, SPAN, width)
    landmarks = jnp.mean(spanned, axis=1, dtype=jnp.float32).astype(jnp.bfloat16)
    picked = jnp.take(spanned, outlier_spans, axis=0).reshape(-1, width)
    query_count = queries.shape[0]
    query_heads = jnp.transpose(queries.reshape(query_count, KVH, GROUP, HEAD), (1, 0, 2, 3))

    def score_rows(shard_rows):
        count_rows = shard_rows.shape[0]
        key_heads = jnp.swapaxes(shard_rows.reshape(count_rows, KVH, HEAD), 0, 1)

        def one_head(pairing):
            query_group, key_group = pairing
            scores = jnp.einsum(
                "qgd,cd->qgc", query_group, key_group, preferred_element_type=jnp.float32
            )
            return (jnp.max(scores, axis=1) * scale_factor).astype(jnp.bfloat16)

        return lax.map(one_head, (query_heads, key_heads))

    landmark_scores = score_rows(lax.all_gather(landmarks, "seq", axis=0, tiled=True))
    outlier_scores = score_rows(lax.all_gather(picked, "seq", axis=0, tiled=True))
    local_gram = lax.dot_general(
        prefill_keys, prefill_keys, (((0,), (0,)), ((), ())), preferred_element_type=jnp.float32
    ) * inverse_tokens
    gram, outlier_scores, landmark_scores = sum_gram(local_gram, outlier_scores, landmark_scores)
    subspace = iterate(gram, start_basis)
    rounded = subspace.astype(jnp.bfloat16)
    coefficients = lax.dot_general(
        rounded, prefill_keys, (((1,), (1,)), ((), ())), preferred_element_type=jnp.float32
    ).astype(jnp.bfloat16)
    return (subspace, coefficients, landmark_scores, outlier_scores)


def solution(mesh):
    placed = (P(("kv", "seq"), None), P("seq", None), P(("kv", "seq")), P())
    return jax.shard_map(
        local,
        mesh=mesh,
        in_specs=placed,
        out_specs=(P(), P(None, ("kv", "seq")), P(None, "seq", "kv"), P(None, "seq", "kv")),
        check_vma=False,
    )
```

```python
import math

import jax
import jax.numpy as jnp
from jax import lax
from jax.experimental import pallas as pl
from jax.experimental.pallas import tpu as pltpu
from jax.sharding import PartitionSpec as P

HI = lax.Precision.HIGHEST
HALF = 128

KVH = 8
HEAD = 128
GROUP = 8
ITERS = 8
SPAN = 8


def _mm(a, b):
    return jnp.dot(a, b, precision=HI, preferred_element_type=jnp.float32)


def _mm_nt(a, b):
    return lax.dot_general(
        a, b, (((1,), (1,)), ((), ())), precision=HI, preferred_element_type=jnp.float32
    )


def _eliminate(a_ref, e_ref):
    n = a_ref.shape[0]
    eye = lax.broadcasted_iota(jnp.int32, (n, n), 0) == lax.broadcasted_iota(jnp.int32, (n, n), 1)
    e_ref[...] = eye.astype(jnp.float32)
    for j in range(n):
        low = (j // 8) * 8
        row_a = a_ref[j:j + 1, :]
        inv = 1.0 / row_a[:, j:j + 1]
        rows = lax.broadcasted_iota(jnp.int32, (n - low, 1), 0) + low
        part = a_ref[low:, :]
        f = jnp.where(rows > j, part[:, j:j + 1] * inv, 0.0)
        a_ref[low:, :] = part - f * row_a
        e_ref[low:, :] = e_ref[low:, :] - f * e_ref[j:j + 1, :]
    diag = jnp.where(eye, a_ref[...], 0.0)
    return jnp.sum(diag, axis=1, keepdims=True), jnp.sum(diag, axis=0, keepdims=True)


def _iterate_kernel(g_ref, s_ref, o_ref, a0_ref, e0_ref, a1_ref, e1_ref):
    o_ref[...] = s_ref[...]

    def step(i, carry):
        product = _mm(o_ref[...], g_ref[...])
        moment = _mm_nt(product, product)
        a0_ref[...] = moment[0:HALF, 0:HALF]
        d0c, d0r = _eliminate(a0_ref, e0_ref)
        e0 = e0_ref[...]
        c = _mm_nt(moment[HALF:, 0:HALF], e0) / d0r
        a1_ref[...] = moment[HALF:, HALF:] - _mm_nt(c * d0r, c)
        d1c, _ = _eliminate(a1_ref, e1_ref)
        q0 = _mm(e0, product[0:HALF, :])
        q1 = _mm(e1_ref[...], product[HALF:, :] - _mm(c, q0))
        o_ref[0:HALF, :] = q0 * lax.rsqrt(d0c)
        o_ref[HALF:, :] = q1 * lax.rsqrt(d1c)
        return carry

    lax.fori_loop(0, ITERS, step, 0)


def iterate(gram, start):
    rank = start.shape[0]
    rest = rank - HALF
    return pl.pallas_call(
        _iterate_kernel,
        out_shape=jax.ShapeDtypeStruct(start.shape, jnp.float32),
        scratch_shapes=[
            pltpu.VMEM((HALF, HALF), jnp.float32),
            pltpu.VMEM((HALF, HALF), jnp.float32),
            pltpu.VMEM((rest, rest), jnp.float32),
            pltpu.VMEM((rest, rest), jnp.float32),
        ],
    )(gram, start)


def _swap(x, flip, axis="seq"):
    return lax.ppermute(x, axis, [(i, i ^ flip) for i in range(lax.axis_size(axis))])


def _halve(x, bit, flip):
    rows = x.shape[0] // 2
    keep = lax.dynamic_slice_in_dim(x, bit * rows, rows)
    send = lax.dynamic_slice_in_dim(x, (1 - bit) * rows, rows)
    return keep + _swap(send, flip)


def _double(x, bit, flip, axis="seq"):
    other = _swap(x, flip, axis)
    rows = x.shape[0]
    out = jnp.zeros((2 * rows,) + x.shape[1:], x.dtype)
    out = lax.dynamic_update_slice_in_dim(out, x, bit * rows, 0)
    return lax.dynamic_update_slice_in_dim(out, other, (1 - bit) * rows, 0)


def sum_gram(local_gram, early, late):
    seq = lax.axis_index("seq")
    kv_size = lax.axis_size("kv")
    core, z_low, z_high = seq % 2, (seq // 2) % 2, (seq // 4) % 2
    s = _halve(local_gram, core, 1)
    s = lax.all_to_all(s.reshape((kv_size, -1) + s.shape[1:]), "kv", 0, 0, tiled=True)
    s, early = lax.optimization_barrier((s, early))
    s = jnp.sum(s, axis=0)
    s = _halve(_halve(s, z_high, 4), z_low, 2)
    s = _double(_double(s, z_low, 2), z_high, 4)
    s = lax.all_gather(s, "kv", axis=0, tiled=True)
    s, late = lax.optimization_barrier((s, late))
    return _double(s, core, 1), early, late


def local(prefill_keys, queries, outlier_spans, start_basis):
    rows_dev = prefill_keys.shape[0]
    width = prefill_keys.shape[1]
    inverse_tokens = 1.0 / (rows_dev * lax.axis_size("kv") * lax.axis_size("seq"))
    scale_factor = 1.0 / math.sqrt(HEAD)
    spanned = prefill_keys.reshape(rows_dev // SPAN, SPAN, width)
    landmarks = jnp.mean(spanned, axis=1, dtype=jnp.float32).astype(jnp.bfloat16)
    picked = jnp.take(spanned, outlier_spans, axis=0).reshape(-1, width)
    query_count = queries.shape[0]
    query_heads = jnp.transpose(queries.reshape(query_count, KVH, GROUP, HEAD), (1, 0, 2, 3))

    def score_rows(shard_rows):
        count_rows = shard_rows.shape[0]
        key_heads = jnp.swapaxes(shard_rows.reshape(count_rows, KVH, HEAD), 0, 1)

        def one_head(pairing):
            query_group, key_group = pairing
            scores = jnp.einsum(
                "qgd,cd->qgc", query_group, key_group, preferred_element_type=jnp.float32
            )
            return (jnp.max(scores, axis=1) * scale_factor).astype(jnp.bfloat16)

        return lax.map(one_head, (query_heads, key_heads))

    gathered = lax.all_gather(jnp.concatenate([landmarks, picked], axis=0), "seq", axis=0)
    span_count = landmarks.shape[0]
    landmark_scores = score_rows(gathered[:, :span_count].reshape(-1, width))
    outlier_scores = score_rows(gathered[:, span_count:].reshape(-1, width))
    local_gram = lax.dot_general(
        prefill_keys, prefill_keys, (((0,), (0,)), ((), ())), preferred_element_type=jnp.float32
    ) * inverse_tokens
    gram, outlier_scores, landmark_scores = sum_gram(local_gram, outlier_scores, landmark_scores)
    subspace = iterate(gram, start_basis)
    rounded = subspace.astype(jnp.bfloat16)
    coefficients = lax.dot_general(
        rounded, prefill_keys, (((1,), (1,)), ((), ())), preferred_element_type=jnp.float32
    ).astype(jnp.bfloat16)
    return (subspace, coefficients, landmark_scores, outlier_scores)


def solution(mesh):
    placed = (P(("kv", "seq"), None), P("seq", None), P(("kv", "seq")), P())
    return jax.shard_map(
        local,
        mesh=mesh,
        in_specs=placed,
        out_specs=(P(), P(None, ("kv", "seq")), P(None, "seq", "kv"), P(None, "seq", "kv")),
        check_vma=False,
    )
```

```python
import math

import jax
import jax.numpy as jnp
from jax import lax
from jax.experimental import pallas as pl
from jax.experimental.pallas import tpu as pltpu
from jax.sharding import PartitionSpec as P

HI = lax.Precision.HIGHEST
HALF = 128

KVH = 8
HEAD = 128
GROUP = 8
ITERS = 8
SPAN = 8


def _mm(a, b):
    return jnp.dot(a, b, precision=HI, preferred_element_type=jnp.float32)


def _mm_nt(a, b):
    return lax.dot_general(
        a, b, (((1,), (1,)), ((), ())), precision=HI, preferred_element_type=jnp.float32
    )


def _eliminate(a_ref, e_ref):
    n = a_ref.shape[0]
    eye = lax.broadcasted_iota(jnp.int32, (n, n), 0) == lax.broadcasted_iota(jnp.int32, (n, n), 1)
    e_ref[...] = eye.astype(jnp.float32)
    for j in range(n):
        low = (j // 8) * 8
        row_a = a_ref[j:j + 1, :]
        inv = 1.0 / row_a[:, j:j + 1]
        rows = lax.broadcasted_iota(jnp.int32, (n - low, 1), 0) + low
        part = a_ref[low:, :]
        f = jnp.where(rows > j, part[:, j:j + 1] * inv, 0.0)
        a_ref[low:, :] = part - f * row_a
        e_ref[low:, :] = e_ref[low:, :] - f * e_ref[j:j + 1, :]
    diag = jnp.where(eye, a_ref[...], 0.0)
    return jnp.sum(diag, axis=1, keepdims=True), jnp.sum(diag, axis=0, keepdims=True)


def _iterate_kernel(g_ref, s_ref, k_ref, o_ref, c_ref, a0_ref, e0_ref, a1_ref, e1_ref, kv_ref, sem):
    keys_in = pltpu.make_async_copy(k_ref, kv_ref, sem)
    keys_in.start()
    o_ref[...] = s_ref[...]

    def step(i, carry):
        product = _mm(o_ref[...], g_ref[...])
        moment = _mm_nt(product, product)
        a0_ref[...] = moment[0:HALF, 0:HALF]
        d0c, d0r = _eliminate(a0_ref, e0_ref)
        e0 = e0_ref[...]
        c = _mm_nt(moment[HALF:, 0:HALF], e0) / d0r
        a1_ref[...] = moment[HALF:, HALF:] - _mm_nt(c * d0r, c)
        d1c, _ = _eliminate(a1_ref, e1_ref)
        q0 = _mm(e0, product[0:HALF, :])
        q1 = _mm(e1_ref[...], product[HALF:, :] - _mm(c, q0))
        o_ref[0:HALF, :] = q0 * lax.rsqrt(d0c)
        o_ref[HALF:, :] = q1 * lax.rsqrt(d1c)
        return carry

    lax.fori_loop(0, ITERS, step, 0)
    keys_in.wait()
    c_ref[...] = lax.dot_general(
        o_ref[...].astype(jnp.bfloat16),
        kv_ref[...],
        (((1,), (1,)), ((), ())),
        preferred_element_type=jnp.float32,
    ).astype(jnp.bfloat16)


def iterate(gram, start, keys):
    rank = start.shape[0]
    rest = rank - HALF
    whole = pl.BlockSpec(memory_space=pltpu.VMEM)
    return pl.pallas_call(
        _iterate_kernel,
        out_shape=(
            jax.ShapeDtypeStruct(start.shape, jnp.float32),
            jax.ShapeDtypeStruct((rank, keys.shape[0]), jnp.bfloat16),
        ),
        in_specs=[whole, whole, pl.BlockSpec(memory_space=pl.ANY)],
        out_specs=(whole, whole),
        scratch_shapes=[
            pltpu.VMEM((HALF, HALF), jnp.float32),
            pltpu.VMEM((HALF, HALF), jnp.float32),
            pltpu.VMEM((rest, rest), jnp.float32),
            pltpu.VMEM((rest, rest), jnp.float32),
            pltpu.VMEM(keys.shape, keys.dtype),
            pltpu.SemaphoreType.DMA(()),
        ],
    )(gram, start, keys)


def _swap(x, flip, axis="seq"):
    return lax.ppermute(x, axis, [(i, i ^ flip) for i in range(lax.axis_size(axis))])


def _halve(x, bit, flip):
    rows = x.shape[0] // 2
    keep = lax.dynamic_slice_in_dim(x, bit * rows, rows)
    send = lax.dynamic_slice_in_dim(x, (1 - bit) * rows, rows)
    return keep + _swap(send, flip)


def _double(x, bit, flip, axis="seq"):
    other = _swap(x, flip, axis)
    rows = x.shape[0]
    out = jnp.zeros((2 * rows,) + x.shape[1:], x.dtype)
    out = lax.dynamic_update_slice_in_dim(out, x, bit * rows, 0)
    return lax.dynamic_update_slice_in_dim(out, other, (1 - bit) * rows, 0)


def sum_gram(local_gram, early, late):
    seq = lax.axis_index("seq")
    kv_size = lax.axis_size("kv")
    core, z_low, z_high = seq % 2, (seq // 2) % 2, (seq // 4) % 2
    s = _halve(local_gram, core, 1)
    s = lax.all_to_all(s.reshape((kv_size, -1) + s.shape[1:]), "kv", 0, 0, tiled=True)
    s, early = lax.optimization_barrier((s, early))
    s = jnp.sum(s, axis=0)
    s = _halve(_halve(s, z_high, 4), z_low, 2)
    s = _double(_double(s, z_low, 2), z_high, 4)
    s = lax.all_gather(s, "kv", axis=0, tiled=True)
    s, late = lax.optimization_barrier((s, late))
    return _double(s, core, 1), early, late


def local(prefill_keys, queries, outlier_spans, start_basis):
    rows_dev = prefill_keys.shape[0]
    width = prefill_keys.shape[1]
    inverse_tokens = 1.0 / (rows_dev * lax.axis_size("kv") * lax.axis_size("seq"))
    scale_factor = 1.0 / math.sqrt(HEAD)
    spanned = prefill_keys.reshape(rows_dev // SPAN, SPAN, width)
    landmarks = jnp.mean(spanned, axis=1, dtype=jnp.float32).astype(jnp.bfloat16)
    picked = jnp.take(spanned, outlier_spans, axis=0).reshape(-1, width)
    query_count = queries.shape[0]
    query_heads = jnp.transpose(queries.reshape(query_count, KVH, GROUP, HEAD), (1, 0, 2, 3))

    def score_rows(shard_rows):
        count_rows = shard_rows.shape[0]
        key_heads = jnp.swapaxes(shard_rows.reshape(count_rows, KVH, HEAD), 0, 1)

        def one_head(pairing):
            query_group, key_group = pairing
            scores = jnp.einsum(
                "qgd,cd->qgc", query_group, key_group, preferred_element_type=jnp.float32
            )
            return (jnp.max(scores, axis=1) * scale_factor).astype(jnp.bfloat16)

        return lax.map(one_head, (query_heads, key_heads))

    landmark_scores = score_rows(lax.all_gather(landmarks, "seq", axis=0, tiled=True))
    outlier_scores = score_rows(lax.all_gather(picked, "seq", axis=0, tiled=True))
    local_gram = lax.dot_general(
        prefill_keys, prefill_keys, (((0,), (0,)), ((), ())), preferred_element_type=jnp.float32
    ) * inverse_tokens
    gram, outlier_scores, landmark_scores = sum_gram(local_gram, outlier_scores, landmark_scores)
    subspace, coefficients = iterate(gram, start_basis, prefill_keys)
    return (subspace, coefficients, landmark_scores, outlier_scores)


def solution(mesh):
    placed = (P(("kv", "seq"), None), P("seq", None), P(("kv", "seq")), P())
    return jax.shard_map(
        local,
        mesh=mesh,
        in_specs=placed,
        out_specs=(P(), P(None, ("kv", "seq")), P(None, "seq", "kv"), P(None, "seq", "kv")),
        check_vma=False,
    )
```

```python
import math

import jax
import jax.numpy as jnp
from jax import lax
from jax.experimental import pallas as pl
from jax.experimental.pallas import tpu as pltpu
from jax.sharding import PartitionSpec as P

HI = lax.Precision.HIGHEST
HALF = 128

KVH = 8
HEAD = 128
GROUP = 8
ITERS = 8
SPAN = 8


def _mm(a, b):
    return jnp.dot(a, b, precision=HI, preferred_element_type=jnp.float32)


def _mm_nt(a, b):
    return lax.dot_general(
        a, b, (((1,), (1,)), ((), ())), precision=HI, preferred_element_type=jnp.float32
    )


def _eliminate(a_ref, e_ref):
    n = a_ref.shape[0]
    eye = lax.broadcasted_iota(jnp.int32, (n, n), 0) == lax.broadcasted_iota(jnp.int32, (n, n), 1)
    e_ref[...] = eye.astype(jnp.float32)
    for j in range(n):
        low = (j // 8) * 8
        row_a = a_ref[j:j + 1, :]
        inv = 1.0 / row_a[:, j:j + 1]
        rows = lax.broadcasted_iota(jnp.int32, (n - low, 1), 0) + low
        part = a_ref[low:, :]
        f = jnp.where(rows > j, part[:, j:j + 1] * inv, 0.0)
        a_ref[low:, :] = part - f * row_a
        e_ref[low:, :] = e_ref[low:, :] - f * e_ref[j:j + 1, :]
    diag = jnp.where(eye, a_ref[...], 0.0)
    return jnp.sum(diag, axis=1, keepdims=True), jnp.sum(diag, axis=0, keepdims=True)


def _iterate_kernel(g_ref, s_ref, k_ref, o_ref, c_ref, a0_ref, e0_ref, a1_ref, e1_ref, kv_ref, sem):
    keys_in = pltpu.make_async_copy(k_ref, kv_ref, sem)
    keys_in.start()
    o_ref[...] = s_ref[...]

    def step(i, carry):
        product = _mm(o_ref[...], g_ref[...])
        moment = _mm_nt(product, product)
        a0_ref[...] = moment[0:HALF, 0:HALF]
        d0c, d0r = _eliminate(a0_ref, e0_ref)
        e0 = e0_ref[...]
        c = _mm_nt(moment[HALF:, 0:HALF], e0) / d0r
        a1_ref[...] = moment[HALF:, HALF:] - _mm_nt(c * d0r, c)
        d1c, _ = _eliminate(a1_ref, e1_ref)
        q0 = _mm(e0, product[0:HALF, :])
        q1 = _mm(e1_ref[...], product[HALF:, :] - _mm(c, q0))
        o_ref[0:HALF, :] = q0 * lax.rsqrt(d0c)
        o_ref[HALF:, :] = q1 * lax.rsqrt(d1c)
        return carry

    lax.fori_loop(0, ITERS, step, 0)
    keys_in.wait()
    c_ref[...] = lax.dot_general(
        o_ref[...].astype(jnp.bfloat16),
        kv_ref[...],
        (((1,), (1,)), ((), ())),
        preferred_element_type=jnp.float32,
    ).astype(jnp.bfloat16)


def iterate(gram, start, keys):
    rank = start.shape[0]
    rest = rank - HALF
    whole = pl.BlockSpec(memory_space=pltpu.VMEM)
    return pl.pallas_call(
        _iterate_kernel,
        out_shape=(
            jax.ShapeDtypeStruct(start.shape, jnp.float32),
            jax.ShapeDtypeStruct((rank, keys.shape[0]), jnp.bfloat16),
        ),
        in_specs=[whole, whole, pl.BlockSpec(memory_space=pl.ANY)],
        out_specs=(whole, whole),
        scratch_shapes=[
            pltpu.VMEM((HALF, HALF), jnp.float32),
            pltpu.VMEM((HALF, HALF), jnp.float32),
            pltpu.VMEM((rest, rest), jnp.float32),
            pltpu.VMEM((rest, rest), jnp.float32),
            pltpu.VMEM(keys.shape, keys.dtype),
            pltpu.SemaphoreType.DMA(()),
        ],
    )(gram, start, keys)


def _swap(x, flip, axis="seq"):
    return lax.ppermute(x, axis, [(i, i ^ flip) for i in range(lax.axis_size(axis))])


def _halve(x, bit, flip):
    rows = x.shape[0] // 2
    keep = lax.dynamic_slice_in_dim(x, bit * rows, rows)
    send = lax.dynamic_slice_in_dim(x, (1 - bit) * rows, rows)
    return keep + _swap(send, flip)


def _double(x, bit, flip, axis="seq"):
    other = _swap(x, flip, axis)
    rows = x.shape[0]
    out = jnp.zeros((2 * rows,) + x.shape[1:], x.dtype)
    out = lax.dynamic_update_slice_in_dim(out, x, bit * rows, 0)
    return lax.dynamic_update_slice_in_dim(out, other, (1 - bit) * rows, 0)


def sum_gram(local_gram, early, late):
    seq = lax.axis_index("seq")
    kv_size = lax.axis_size("kv")
    core, z_low, z_high = seq % 2, (seq // 2) % 2, (seq // 4) % 2
    keep, send = local_gram
    s = keep + _swap(send, 1)
    s = lax.all_to_all(s.reshape((kv_size, -1) + s.shape[1:]), "kv", 0, 0, tiled=True)
    s, early = lax.optimization_barrier((s, early))
    s = jnp.sum(s, axis=0)
    s = _halve(_halve(s, z_high, 4), z_low, 2)
    s = _double(_double(s, z_low, 2), z_high, 4)
    s = lax.all_gather(s, "kv", axis=0, tiled=True)
    s, late = lax.optimization_barrier((s, late))
    return _double(s, core, 1), early, late


def local(prefill_keys, queries, outlier_spans, start_basis):
    rows_dev = prefill_keys.shape[0]
    width = prefill_keys.shape[1]
    inverse_tokens = 1.0 / (rows_dev * lax.axis_size("kv") * lax.axis_size("seq"))
    scale_factor = 1.0 / math.sqrt(HEAD)
    spanned = prefill_keys.reshape(rows_dev // SPAN, SPAN, width)
    landmarks = jnp.mean(spanned, axis=1, dtype=jnp.float32).astype(jnp.bfloat16)
    picked = jnp.take(spanned, outlier_spans, axis=0).reshape(-1, width)
    query_count = queries.shape[0]
    query_heads = jnp.transpose(queries.reshape(query_count, KVH, GROUP, HEAD), (1, 0, 2, 3))

    def score_rows(shard_rows):
        count_rows = shard_rows.shape[0]
        key_heads = jnp.swapaxes(shard_rows.reshape(count_rows, KVH, HEAD), 0, 1)

        def one_head(pairing):
            query_group, key_group = pairing
            scores = jnp.einsum(
                "qgd,cd->qgc", query_group, key_group, preferred_element_type=jnp.float32
            )
            return (jnp.max(scores, axis=1) * scale_factor).astype(jnp.bfloat16)

        return lax.map(one_head, (query_heads, key_heads))

    landmark_scores = score_rows(lax.all_gather(landmarks, "seq", axis=0, tiled=True))
    outlier_scores = score_rows(lax.all_gather(picked, "seq", axis=0, tiled=True))
    half = width // 2
    core = lax.axis_index("seq") % 2

    def gram_rows(start):
        cols = lax.dynamic_slice_in_dim(prefill_keys, start, half, axis=1)
        return lax.dot_general(
            cols, prefill_keys, (((0,), (0,)), ((), ())), preferred_element_type=jnp.float32
        ) * inverse_tokens

    local_gram = (gram_rows(core * half), gram_rows((1 - core) * half))
    gram, outlier_scores, landmark_scores = sum_gram(local_gram, outlier_scores, landmark_scores)
    subspace, coefficients = iterate(gram, start_basis, prefill_keys)
    return (subspace, coefficients, landmark_scores, outlier_scores)


def solution(mesh):
    placed = (P(("kv", "seq"), None), P("seq", None), P(("kv", "seq")), P())
    return jax.shard_map(
        local,
        mesh=mesh,
        in_specs=placed,
        out_specs=(P(), P(None, ("kv", "seq")), P(None, "seq", "kv"), P(None, "seq", "kv")),
        check_vma=False,
    )
```

```python
import math

import jax
import jax.numpy as jnp
from jax import lax
from jax.experimental import pallas as pl
from jax.experimental.pallas import tpu as pltpu
from jax.sharding import PartitionSpec as P

HI = lax.Precision.HIGHEST
HALF = 128

KVH = 8
HEAD = 128
GROUP = 8
ITERS = 8
SPAN = 8


def _mm(a, b):
    return jnp.dot(a, b, precision=HI, preferred_element_type=jnp.float32)


def _mm_nt(a, b):
    return lax.dot_general(
        a, b, (((1,), (1,)), ((), ())), precision=HI, preferred_element_type=jnp.float32
    )


def _eliminate(a_ref, e_ref):
    n = a_ref.shape[0]
    eye = lax.broadcasted_iota(jnp.int32, (n, n), 0) == lax.broadcasted_iota(jnp.int32, (n, n), 1)
    e_ref[...] = eye.astype(jnp.float32)
    for j in range(n):
        low = (j // 8) * 8
        row_a = a_ref[j:j + 1, :]
        inv = 1.0 / row_a[:, j:j + 1]
        rows = lax.broadcasted_iota(jnp.int32, (n - low, 1), 0) + low
        part = a_ref[low:, :]
        f = jnp.where(rows > j, part[:, j:j + 1] * inv, 0.0)
        a_ref[low:, :] = part - f * row_a
        e_ref[low:, :] = e_ref[low:, :] - f * e_ref[j:j + 1, :]
    diag = jnp.where(eye, a_ref[...], 0.0)
    return jnp.sum(diag, axis=1, keepdims=True), jnp.sum(diag, axis=0, keepdims=True)


def _iterate_kernel(g_ref, s_ref, k_ref, o_ref, c_ref, a0_ref, e0_ref, a1_ref, e1_ref, kv_ref, sem):
    keys_in = pltpu.make_async_copy(k_ref, kv_ref, sem)
    keys_in.start()
    o_ref[...] = s_ref[...]

    def step(i, carry):
        product = _mm(o_ref[...], g_ref[...])
        moment = _mm_nt(product, product)
        a0_ref[...] = moment[0:HALF, 0:HALF]
        d0c, d0r = _eliminate(a0_ref, e0_ref)
        e0 = e0_ref[...]
        c = _mm_nt(moment[HALF:, 0:HALF], e0) / d0r
        a1_ref[...] = moment[HALF:, HALF:] - _mm_nt(c * d0r, c)
        d1c, _ = _eliminate(a1_ref, e1_ref)
        q0 = _mm(e0, product[0:HALF, :])
        q1 = _mm(e1_ref[...], product[HALF:, :] - _mm(c, q0))
        o_ref[0:HALF, :] = q0 * lax.rsqrt(d0c)
        o_ref[HALF:, :] = q1 * lax.rsqrt(d1c)
        return carry

    lax.fori_loop(0, ITERS, step, 0)
    keys_in.wait()
    c_ref[...] = lax.dot_general(
        o_ref[...].astype(jnp.bfloat16),
        kv_ref[...],
        (((1,), (1,)), ((), ())),
        preferred_element_type=jnp.float32,
    ).astype(jnp.bfloat16)


def iterate(gram, start, keys):
    rank = start.shape[0]
    rest = rank - HALF
    whole = pl.BlockSpec(memory_space=pltpu.VMEM)
    return pl.pallas_call(
        _iterate_kernel,
        out_shape=(
            jax.ShapeDtypeStruct(start.shape, jnp.float32),
            jax.ShapeDtypeStruct((rank, keys.shape[0]), jnp.bfloat16),
        ),
        in_specs=[whole, whole, pl.BlockSpec(memory_space=pl.ANY)],
        out_specs=(whole, whole),
        scratch_shapes=[
            pltpu.VMEM((HALF, HALF), jnp.float32),
            pltpu.VMEM((HALF, HALF), jnp.float32),
            pltpu.VMEM((rest, rest), jnp.float32),
            pltpu.VMEM((rest, rest), jnp.float32),
            pltpu.VMEM(keys.shape, keys.dtype),
            pltpu.SemaphoreType.DMA(()),
        ],
    )(gram, start, keys)


def _swap(x, flip, axis="seq"):
    return lax.ppermute(x, axis, [(i, i ^ flip) for i in range(lax.axis_size(axis))])


def _halve(x, bit, flip):
    rows = x.shape[0] // 2
    keep = lax.dynamic_slice_in_dim(x, bit * rows, rows)
    send = lax.dynamic_slice_in_dim(x, (1 - bit) * rows, rows)
    return keep + _swap(send, flip)


def _double(x, bit, flip, axis="seq"):
    other = _swap(x, flip, axis)
    rows = x.shape[0]
    out = jnp.zeros((2 * rows,) + x.shape[1:], x.dtype)
    out = lax.dynamic_update_slice_in_dim(out, x, bit * rows, 0)
    return lax.dynamic_update_slice_in_dim(out, other, (1 - bit) * rows, 0)


def sum_gram(local_gram, early, late):
    seq = lax.axis_index("seq")
    kv_size = lax.axis_size("kv")
    core, z_low, z_high = seq % 2, (seq // 2) % 2, (seq // 4) % 2
    keep, send = local_gram
    s = keep + _swap(send, 1)
    s = lax.all_to_all(s.reshape((kv_size, -1) + s.shape[1:]), "kv", 0, 0, tiled=True)
    s, early = lax.optimization_barrier((s, early))
    s = jnp.sum(s, axis=0)
    s = _halve(_halve(s, z_high, 4), z_low, 2)
    s = _double(_double(s, z_low, 2), z_high, 4)
    s = lax.all_gather(s, "kv", axis=0, tiled=True)
    s, late = lax.optimization_barrier((s, late))
    return _double(s, core, 1), early, late


def local(prefill_keys, queries, outlier_spans, start_basis):
    rows_dev = prefill_keys.shape[0]
    width = prefill_keys.shape[1]
    inverse_tokens = 1.0 / (rows_dev * lax.axis_size("kv") * lax.axis_size("seq"))
    scale_factor = 1.0 / math.sqrt(HEAD)
    spanned = prefill_keys.reshape(rows_dev // SPAN, SPAN, width)
    span_of_row = lax.broadcasted_iota(jnp.int32, (rows_dev // SPAN, rows_dev), 1) // SPAN
    span_index = lax.broadcasted_iota(jnp.int32, (rows_dev // SPAN, rows_dev), 0)
    averaging = jnp.where(span_of_row == span_index, 1.0 / SPAN, 0.0).astype(jnp.bfloat16)
    landmarks = jnp.dot(averaging, prefill_keys, preferred_element_type=jnp.float32).astype(
        jnp.bfloat16
    )
    picked = jnp.take(spanned, outlier_spans, axis=0).reshape(-1, width)
    query_count = queries.shape[0]
    query_heads = jnp.transpose(queries.reshape(query_count, KVH, GROUP, HEAD), (1, 0, 2, 3))

    def score_rows(shard_rows):
        count_rows = shard_rows.shape[0]
        key_heads = jnp.swapaxes(shard_rows.reshape(count_rows, KVH, HEAD), 0, 1)

        def one_head(pairing):
            query_group, key_group = pairing
            scores = jnp.einsum(
                "qgd,cd->qgc", query_group, key_group, preferred_element_type=jnp.float32
            )
            return (jnp.max(scores, axis=1) * scale_factor).astype(jnp.bfloat16)

        return lax.map(one_head, (query_heads, key_heads))

    landmark_scores = score_rows(lax.all_gather(landmarks, "seq", axis=0, tiled=True))
    outlier_scores = score_rows(lax.all_gather(picked, "seq", axis=0, tiled=True))
    half = width // 2
    core = lax.axis_index("seq") % 2

    def gram_rows(start):
        cols = lax.dynamic_slice_in_dim(prefill_keys, start, half, axis=1)
        return lax.dot_general(
            cols, prefill_keys, (((0,), (0,)), ((), ())), preferred_element_type=jnp.float32
        ) * inverse_tokens

    local_gram = (gram_rows(core * half), gram_rows((1 - core) * half))
    gram, outlier_scores, landmark_scores = sum_gram(local_gram, outlier_scores, landmark_scores)
    subspace, coefficients = iterate(gram, start_basis, prefill_keys)
    return (subspace, coefficients, landmark_scores, outlier_scores)


def solution(mesh):
    placed = (P(("kv", "seq"), None), P("seq", None), P(("kv", "seq")), P())
    return jax.shard_map(
        local,
        mesh=mesh,
        in_specs=placed,
        out_specs=(P(), P(None, ("kv", "seq")), P(None, "seq", "kv"), P(None, "seq", "kv")),
        check_vma=False,
    )
```

```python
import math

import jax
import jax.numpy as jnp
from jax import lax
from jax.experimental import pallas as pl
from jax.experimental.pallas import tpu as pltpu
from jax.sharding import PartitionSpec as P

HI = lax.Precision.HIGHEST
HALF = 128

KVH = 8
HEAD = 128
GROUP = 8
ITERS = 8
SPAN = 8


def _mm(a, b):
    return jnp.dot(a, b, precision=HI, preferred_element_type=jnp.float32)


def _mm_nt(a, b):
    return lax.dot_general(
        a, b, (((1,), (1,)), ((), ())), precision=HI, preferred_element_type=jnp.float32
    )


def _eliminate(a_ref, e_ref):
    n = a_ref.shape[0]
    eye = lax.broadcasted_iota(jnp.int32, (n, n), 0) == lax.broadcasted_iota(jnp.int32, (n, n), 1)
    e_ref[...] = eye.astype(jnp.float32)
    for j in range(n):
        low = (j // 8) * 8
        row_a = a_ref[j:j + 1, :]
        inv = 1.0 / row_a[:, j:j + 1]
        rows = lax.broadcasted_iota(jnp.int32, (n - low, 1), 0) + low
        part = a_ref[low:, :]
        f = jnp.where(rows > j, part[:, j:j + 1] * inv, 0.0)
        a_ref[low:, :] = part - f * row_a
        e_ref[low:, :] = e_ref[low:, :] - f * e_ref[j:j + 1, :]
    diag = jnp.where(eye, a_ref[...], 0.0)
    return jnp.sum(diag, axis=1, keepdims=True), jnp.sum(diag, axis=0, keepdims=True)


def _iterate_kernel(g_ref, s_ref, k_ref, o_ref, c_ref, a0_ref, e0_ref, a1_ref, e1_ref, kv_ref, sem):
    keys_in = pltpu.make_async_copy(k_ref, kv_ref, sem)
    keys_in.start()
    o_ref[...] = s_ref[...]

    def step(i, carry):
        product = _mm(o_ref[...], g_ref[...])
        moment = _mm_nt(product, product)
        a0_ref[...] = moment[0:HALF, 0:HALF]
        d0c, d0r = _eliminate(a0_ref, e0_ref)
        e0 = e0_ref[...]
        c = _mm_nt(moment[HALF:, 0:HALF], e0) / d0r
        a1_ref[...] = moment[HALF:, HALF:] - _mm_nt(c * d0r, c)
        d1c, _ = _eliminate(a1_ref, e1_ref)
        q0 = _mm(e0, product[0:HALF, :])
        q1 = _mm(e1_ref[...], product[HALF:, :] - _mm(c, q0))
        o_ref[0:HALF, :] = q0 * lax.rsqrt(d0c)
        o_ref[HALF:, :] = q1 * lax.rsqrt(d1c)
        return carry

    lax.fori_loop(0, ITERS, step, 0)
    keys_in.wait()
    c_ref[...] = lax.dot_general(
        o_ref[...].astype(jnp.bfloat16),
        kv_ref[...],
        (((1,), (1,)), ((), ())),
        preferred_element_type=jnp.float32,
    ).astype(jnp.bfloat16)


def iterate(gram, start, keys):
    rank = start.shape[0]
    rest = rank - HALF
    whole = pl.BlockSpec(memory_space=pltpu.VMEM)
    return pl.pallas_call(
        _iterate_kernel,
        out_shape=(
            jax.ShapeDtypeStruct(start.shape, jnp.float32),
            jax.ShapeDtypeStruct((rank, keys.shape[0]), jnp.bfloat16),
        ),
        in_specs=[whole, whole, pl.BlockSpec(memory_space=pl.ANY)],
        out_specs=(whole, whole),
        scratch_shapes=[
            pltpu.VMEM((HALF, HALF), jnp.float32),
            pltpu.VMEM((HALF, HALF), jnp.float32),
            pltpu.VMEM((rest, rest), jnp.float32),
            pltpu.VMEM((rest, rest), jnp.float32),
            pltpu.VMEM(keys.shape, keys.dtype),
            pltpu.SemaphoreType.DMA(()),
        ],
    )(gram, start, keys)


def _swap(x, flip, axis="seq"):
    return lax.ppermute(x, axis, [(i, i ^ flip) for i in range(lax.axis_size(axis))])


def _halve(x, bit, flip):
    rows = x.shape[0] // 2
    keep = lax.dynamic_slice_in_dim(x, bit * rows, rows)
    send = lax.dynamic_slice_in_dim(x, (1 - bit) * rows, rows)
    return keep + _swap(send, flip)


def _double(x, bit, flip, axis="seq"):
    other = _swap(x, flip, axis)
    rows = x.shape[0]
    out = jnp.zeros((2 * rows,) + x.shape[1:], x.dtype)
    out = lax.dynamic_update_slice_in_dim(out, x, bit * rows, 0)
    return lax.dynamic_update_slice_in_dim(out, other, (1 - bit) * rows, 0)


def sum_gram(local_gram, early, late):
    seq = lax.axis_index("seq")
    kv_size = lax.axis_size("kv")
    core, z_low, z_high = seq % 2, (seq // 2) % 2, (seq // 4) % 2
    keep, send = local_gram
    s = keep + _swap(send, 1)
    s = lax.all_to_all(s.reshape((kv_size, -1) + s.shape[1:]), "kv", 0, 0, tiled=True)
    s, early = lax.optimization_barrier((s, early))
    s = jnp.sum(s, axis=0)
    s = _halve(_halve(s, z_high, 4), z_low, 2)
    s = _double(_double(s, z_low, 2), z_high, 4)
    s = lax.all_gather(s, "kv", axis=0, tiled=True)
    s, late = lax.optimization_barrier((s, late))
    return _double(s, core, 1), early, late


def local(prefill_keys, queries, outlier_spans, start_basis):
    rows_dev = prefill_keys.shape[0]
    width = prefill_keys.shape[1]
    inverse_tokens = 1.0 / (rows_dev * lax.axis_size("kv") * lax.axis_size("seq"))
    scale_factor = 1.0 / math.sqrt(HEAD)
    spanned = prefill_keys.reshape(rows_dev // SPAN, SPAN, width)
    span_of_row = lax.broadcasted_iota(jnp.int32, (rows_dev // SPAN, rows_dev), 1) // SPAN
    span_index = lax.broadcasted_iota(jnp.int32, (rows_dev // SPAN, rows_dev), 0)
    averaging = jnp.where(span_of_row == span_index, 1.0 / SPAN, 0.0).astype(jnp.bfloat16)
    landmarks = jnp.dot(averaging, prefill_keys, preferred_element_type=jnp.float32).astype(
        jnp.bfloat16
    )
    picked = jnp.concatenate(
        [
            lax.dynamic_slice_in_dim(prefill_keys, outlier_spans[entry] * SPAN, SPAN)
            for entry in range(outlier_spans.shape[0])
        ],
        axis=0,
    )
    query_count = queries.shape[0]
    query_heads = jnp.transpose(queries.reshape(query_count, KVH, GROUP, HEAD), (1, 0, 2, 3))

    def score_rows(shard_rows):
        count_rows = shard_rows.shape[0]
        key_heads = jnp.swapaxes(shard_rows.reshape(count_rows, KVH, HEAD), 0, 1)

        def one_head(pairing):
            query_group, key_group = pairing
            scores = jnp.einsum(
                "qgd,cd->qgc", query_group, key_group, preferred_element_type=jnp.float32
            )
            return (jnp.max(scores, axis=1) * scale_factor).astype(jnp.bfloat16)

        return lax.map(one_head, (query_heads, key_heads))

    landmark_scores = score_rows(lax.all_gather(landmarks, "seq", axis=0, tiled=True))
    outlier_scores = score_rows(lax.all_gather(picked, "seq", axis=0, tiled=True))
    half = width // 2
    core = lax.axis_index("seq") % 2

    def gram_rows(start):
        cols = lax.dynamic_slice_in_dim(prefill_keys, start, half, axis=1)
        return lax.dot_general(
            cols, prefill_keys, (((0,), (0,)), ((), ())), preferred_element_type=jnp.float32
        ) * inverse_tokens

    local_gram = (gram_rows(core * half), gram_rows((1 - core) * half))
    gram, outlier_scores, landmark_scores = sum_gram(local_gram, outlier_scores, landmark_scores)
    subspace, coefficients = iterate(gram, start_basis, prefill_keys)
    return (subspace, coefficients, landmark_scores, outlier_scores)


def solution(mesh):
    placed = (P(("kv", "seq"), None), P("seq", None), P(("kv", "seq")), P())
    return jax.shard_map(
        local,
        mesh=mesh,
        in_specs=placed,
        out_specs=(P(), P(None, ("kv", "seq")), P(None, "seq", "kv"), P(None, "seq", "kv")),
        check_vma=False,
    )
```
